32 devices in a mesh: dp: 4 (over x, core), expert: 8 (over z, y).
Axes of the slice: x: 2, y: 2, z: 4, core: 2. Of those that a mesh axis runs over, the one named last changes fastest.
Arguments:
- inputs: bfloat16 [512, 4096], P(('dp', 'expert')), may hold values from -6 to 6
- grad_out: bfloat16 [512, 4096], P(('dp', 'expert')), may hold values from -0.796875 to 0.796875
- labels: int32 [512, 1], P(('dp', 'expert')), may hold values from 0 to 7; in each aligned block of 16 rows (0 to 15, 16 to 31, ...) at most 3 rows name the same one
- w_gate: bfloat16 [4096, 57344], P('dp', 'expert'), may hold values from -0.09375 to 0.09375
- w_up: bfloat16 [4096, 57344], P('dp', 'expert'), may hold values from -0.09375 to 0.09375
- w_down: bfloat16 [57344, 4096], P('expert', 'dp'), may hold values from -0.0625 to 0.0625
Outputs:
- grad_in: bfloat16 [512, 4096], P(('dp', 'expert'))
- grad_gate: bfloat16 [4096, 57344], P('dp', 'expert')
- grad_up: bfloat16 [4096, 57344], P('dp', 'expert')
- grad_down: bfloat16 [57344, 4096], P('expert', 'dp')
The draws below stay inside these ranges and needn't reach their ends.
Inputs may be any that keep to these rules, and one draw needn't show every extreme that they name: `labels`: among the 16 rows of one device no expert is named by more than 3 rows, a bound that some block reaches.
All inputs are finite; a program needn't handle non-finite values.
Results may differ from the reference program's by a relative error of at most 0.011.
Values may be sent and summed in bfloat16 or wider, within the bound.
No kernel may reach another device: no remote copies, remote signals or barrier semaphores. Data moves between devices by JAX's collectives and lax.ppermute only.
A program may use at most 192 MiB of HBM per device.

```python
import math
import jax
import jax.numpy as jnp
import numpy as np
from jax import lax

D = 4096
FF = 7168
EXPERTS = 8
TOK_DEV = 16
CAP = 3
ROWS = 96
TOKENS = 512


def levels(key, extent, pieces, smallest, largest):
    def one(axis_at, shards_of):
        draws = jax.random.uniform(jax.random.fold_in(jax.random.fold_in(key, 6), axis_at), (shards_of,), jnp.float32, smallest / len(pieces), largest / len(pieces))
        return jnp.repeat(jnp.exp(draws), extent[axis_at] // shards_of).reshape((-1,) + (1,) * (len(extent) - axis_at - 1))

    factor_of = one(*pieces[0])
    for cut in pieces[1:]:
        factor_of = factor_of * one(*cut)
    return factor_of


def assign_block(rng, own, number, rows, count, top, most, lean):
    ranking = jax.random.permutation(rng, count)
    packed, common = load_shares(count, rows * top, most, lean, True), load_shares(count, rows * top, most, lean, False)
    places = jnp.arange(count)

    def named(tallies, turn):
        used = int((tallies > 0).sum())
        fixed = max(1, used // 4)
        passed = fixed + (places - fixed + turn * (used - fixed)) % max(1, count - fixed)
        return jnp.zeros((count,), jnp.int32).at[ranking[jnp.where(places < fixed, places, passed)]].set(jnp.asarray(tallies, jnp.int32))

    tallies = jnp.where(number % 4 == 0, named(packed, number // 4), named(common, number - number // 4 - 1))
    mixed = jax.random.permutation(jax.random.fold_in(own, 3), count)
    donor, receiver = mixed[0:count // 2 * 2:2], mixed[1:count // 2 * 2:2]
    margin = jnp.minimum(tallies[donor] - 1, most - tallies[receiver]) // 2
    margin = jnp.where((donor == ranking[0]) | (receiver == ranking[0]) | (tallies[receiver] == 0), 0, jnp.maximum(margin, 0))
    passed = jax.random.randint(jax.random.fold_in(own, 4), (count // 2,), 0, 1 << 20) % (margin + 1)
    tallies = tallies.at[donor].add(-passed).at[receiver].add(passed)
    items = jnp.searchsorted(jnp.cumsum(tallies), jnp.arange(rows * top), side="right").astype(jnp.int32)
    listing = items.reshape(top, rows).T
    listing = listing[jax.random.permutation(jax.random.fold_in(own, 1), rows)]
    turn = jax.random.randint(jax.random.fold_in(own, 2), (rows, 1), 0, top)
    return jnp.take_along_axis(listing, (jnp.arange(top)[None, :] + turn) % top, axis=1)


def load_shares(amount, total, limit, lean, full):
    loads = [(1 << 20) // math.isqrt(grade ** lean) + 1 for grade in range(1, amount + 1)]
    largest = limit if full else min(limit, max(-(-total // amount), total * loads[0] // sum(loads)))
    least = 1 if total - largest >= amount - 1 else 0
    holding, rest = [largest] + [least] * (amount - 1), total - largest - least * (amount - 1)
    while rest > 0:
        candidates = [i for i in range(1, amount) if holding[i] < largest] or [i for i in range(1, amount) if holding[i] < limit]
        whole, budget = sum([loads[i] for i in candidates]), rest
        for i in candidates:
            addition = min(limit - holding[i], max(1, budget * loads[i] // whole), rest)
            holding[i] = holding[i] + addition
            rest = rest - addition
    return np.array(holding)


def bell_draw(stream_key, shape, deviation, limit, pieces=(), kind=jnp.bfloat16):
    drawn = jax.random.normal(stream_key, shape, jnp.float32) * deviation
    if len(pieces) > 0:
        drawn = levels(stream_key, shape, pieces, -0.22, 0.18) * drawn
    return jnp.clip(drawn, min=-limit, max=limit).astype(kind)


def setup_inputs(seed: int = 0) -> dict:
    arg_keys = jax.random.split(jax.random.key(seed), 7)
    inputs = bell_draw(arg_keys[0], (TOKENS, D), 1.0, 6.0, ((0, 32),))
    grad_out = bell_draw(arg_keys[1], (TOKENS, D), 0.1, 0.796875, ((0, 32),))
    labels_keys = jax.random.split(jax.random.fold_in(arg_keys[2], 1), TOKENS // TOK_DEV)
    labels_turns = jax.random.permutation(jax.random.fold_in(arg_keys[2], 3), TOKENS // TOK_DEV)
    labels = jax.vmap(lambda own, number: assign_block(jax.random.fold_in(arg_keys[2], 2), own, number, TOK_DEV, EXPERTS, 1, CAP, 2))(labels_keys, labels_turns).reshape((TOKENS, 1))
    w_gate = bell_draw(arg_keys[3], (D, EXPERTS * FF), D ** -0.5, 0.09375, ((0, 4), (1, 8)))
    w_up = bell_draw(arg_keys[4], (D, EXPERTS * FF), D ** -0.5, 0.09375, ((0, 4), (1, 8)))
    w_down = bell_draw(arg_keys[5], (EXPERTS * FF, D), FF ** -0.5, 0.0625, ((0, 8), (1, 4)))
    return {"inputs": inputs, "grad_out": grad_out, "labels": labels, "w_gate": w_gate, "w_up": w_up, "w_down": w_down}


def expert_backward(rows_in, rows_grad, gate_mat, up_mat, down_mat):
    gate = jnp.dot(rows_in, gate_mat, preferred_element_type=jnp.float32)
    up = jnp.dot(rows_in, up_mat, preferred_element_type=jnp.float32)
    sig = jax.nn.sigmoid(gate)
    act = gate * sig
    hidden = (act * up).astype(jnp.bfloat16)
    dhid = jnp.dot(rows_grad, down_mat.T, preferred_element_type=jnp.float32)
    d_up = (dhid * act).astype(jnp.bfloat16)
    d_gate = (dhid * up * sig * (1.0 + gate * (1.0 - sig))).astype(jnp.bfloat16)
    d_in = jnp.dot(d_gate, gate_mat.T, preferred_element_type=jnp.float32)
    d_in = (d_in + jnp.dot(d_up, up_mat.T, preferred_element_type=jnp.float32)).astype(jnp.bfloat16)
    g_gate = jnp.dot(rows_in.T, d_gate, preferred_element_type=jnp.float32).astype(jnp.bfloat16)
    g_up = jnp.dot(rows_in.T, d_up, preferred_element_type=jnp.float32).astype(jnp.bfloat16)
    g_down = jnp.dot(hidden.T, rows_grad, preferred_element_type=jnp.float32).astype(jnp.bfloat16)
    return d_in, g_gate, g_up, g_down


def reference(inputs, grad_out, labels, w_gate, w_up, w_down):
    label_col = labels[:, 0]
    order = jnp.argsort(label_col, stable=True).astype(jnp.int32)
    counts = jnp.sum((label_col[:, None] == jnp.arange(EXPERTS, dtype=jnp.int32)[None, :]).astype(jnp.int32), axis=0)
    offsets = (jnp.cumsum(counts) - counts).astype(jnp.int32)
    lanes = jnp.arange(ROWS, dtype=jnp.int32)

    def one_expert(expert_id):
        valid = lanes < counts[expert_id]
        where_sorted = jnp.minimum(offsets[expert_id] + lanes, TOKENS - 1).astype(jnp.int32)
        token_ids = order[where_sorted]
        rows_in = jnp.where(valid[:, None], inputs[token_ids], jnp.zeros((), jnp.bfloat16))
        rows_grad = jnp.where(valid[:, None], grad_out[token_ids], jnp.zeros((), jnp.bfloat16))
        start = (expert_id * FF).astype(jnp.int32)
        gate_mat = lax.dynamic_slice_in_dim(w_gate, start, FF, 1)
        up_mat = lax.dynamic_slice_in_dim(w_up, start, FF, 1)
        down_mat = lax.dynamic_slice_in_dim(w_down, start, FF, 0)
        d_in, g_gate, g_up, g_down = expert_backward(rows_in, rows_grad, gate_mat, up_mat, down_mat)
        targets = jnp.where(valid, token_ids, TOKENS).astype(jnp.int32)
        return g_gate, g_up, g_down, d_in, targets

    g_gate, g_up, g_down, d_rows, targets = lax.map(one_expert, jnp.arange(EXPERTS, dtype=jnp.int32))
    grad_gate = jnp.transpose(g_gate, (1, 0, 2)).reshape(D, EXPERTS * FF)
    grad_up = jnp.transpose(g_up, (1, 0, 2)).reshape(D, EXPERTS * FF)
    grad_down = g_down.reshape(EXPERTS * FF, D)
    grad_in = jnp.zeros((TOKENS, D), jnp.bfloat16).at[targets.reshape(-1)].set(d_rows.reshape(-1, D), mode="drop")
    return grad_in, grad_gate, grad_up, grad_down
```

```python
import jax
import jax.numpy as jnp
from jax import lax
from jax.sharding import PartitionSpec as P

EXPERTS = 8
ALL = ("dp", "expert")


def nonlinear(gate, up, dhid):
    sig = jax.nn.sigmoid(gate)
    act = gate * sig
    hidden = (act * up).astype(jnp.bfloat16)
    d_up = (dhid * act).astype(jnp.bfloat16)
    d_gate = (dhid * up * sig * (1.0 + gate * (1.0 - sig))).astype(jnp.bfloat16)
    return (hidden, d_up, d_gate)


def contract_rows(left, right):
    return lax.dot_general(
        left, right, (((0,), (0,)), ((), ())), preferred_element_type=jnp.float32
    )


def on_device(inputs, grad_out, labels, w_gate, w_up, w_down):
    members = lax.axis_size("expert")
    replicas = lax.axis_size("dp")
    group = members // EXPERTS
    tok_count = inputs.shape[0]
    width = inputs.shape[1]
    columns = width // replicas
    capacity = 3 * tok_count // (2 * EXPERTS)
    label_col = labels[:, 0]
    onehot = (label_col[:, None] == jnp.arange(EXPERTS, dtype=jnp.int32)[None, :]).astype(jnp.int32)
    before = jnp.cumsum(onehot, axis=0) - onehot
    rank_in = jnp.sum(before * onehot, axis=1)
    slot_ids = label_col * capacity + rank_in

    both = jnp.stack([inputs, grad_out])
    slots = jnp.zeros((2, EXPERTS * capacity, width), jnp.bfloat16).at[:, slot_ids].set(both)
    send = slots.reshape(2, EXPERTS, capacity, replicas, columns)
    send = jnp.transpose(send, (3, 1, 0, 2, 4))
    send = jnp.broadcast_to(
        send[:, :, None], (replicas, EXPERTS, group, 2, capacity, columns)
    ).reshape(replicas * members, 2 * capacity * columns)
    recv = lax.all_to_all(send, ALL, 0, 0, tiled=True)
    recv = recv.reshape(replicas * members, 2, capacity, columns)
    rows_in = recv[:, 0].reshape(-1, columns)
    rows_grad = recv[:, 1].reshape(-1, columns)

    gate_part = jnp.dot(rows_in, w_gate, preferred_element_type=jnp.float32)
    up_part = jnp.dot(rows_in, w_up, preferred_element_type=jnp.float32)
    dhid_part = lax.dot_general(
        rows_grad, w_down, (((1,), (1,)), ((), ())), preferred_element_type=jnp.float32
    )
    parts = jnp.stack([gate_part, up_part, dhid_part])
    reduced = lax.psum_scatter(parts, "dp", scatter_dimension=2, tiled=True)
    hidden, d_up, d_gate = nonlinear(reduced[0], reduced[1], reduced[2])
    gathered = lax.all_gather(jnp.stack([hidden, d_up, d_gate]), "dp", axis=2, tiled=True)
    hidden, d_up, d_gate = gathered[0], gathered[1], gathered[2]

    d_rows = lax.dot_general(
        d_gate, w_gate, (((1,), (1,)), ((), ())), preferred_element_type=jnp.float32
    )
    d_rows = d_rows + lax.dot_general(
        d_up, w_up, (((1,), (1,)), ((), ())), preferred_element_type=jnp.float32
    )
    back = d_rows.astype(jnp.bfloat16).reshape(replicas * members, capacity * columns)
    back = lax.all_to_all(back, ALL, 0, 0, tiled=True)
    back = back.reshape(replicas, EXPERTS, group, capacity, columns).astype(jnp.float32)
    summed = jnp.sum(back, axis=2)
    summed = jnp.transpose(summed, (1, 2, 0, 3)).reshape(EXPERTS * capacity, width)
    grad_in = summed[slot_ids].astype(jnp.bfloat16)
    grad_gate = contract_rows(rows_in, d_gate).astype(jnp.bfloat16)
    grad_up = contract_rows(rows_in, d_up).astype(jnp.bfloat16)
    grad_down = contract_rows(hidden, rows_grad).astype(jnp.bfloat16)
    return (grad_in, grad_gate, grad_up, grad_down)


def solution(mesh):
    return jax.shard_map(
        on_device,
        mesh=mesh,
        in_specs=(
            P(ALL, None),
            P(ALL, None),
            P(ALL, None),
            P("dp", "expert"),
            P("dp", "expert"),
            P("expert", "dp"),
        ),
        out_specs=(
            P(ALL, None),
            P("dp", "expert"),
            P("dp", "expert"),
            P("expert", "dp"),
        ),
        check_vma=False,
    )
```

```python
import jax
import jax.numpy as jnp
from jax import lax
from jax.sharding import PartitionSpec as P

EXPERTS = 8
ALL = ("dp", "expert")


def nonlinear(gate, up, dhid):
    sig = jax.nn.sigmoid(gate)
    act = gate * sig
    hidden = (act * up).astype(jnp.bfloat16)
    d_up = (dhid * act).astype(jnp.bfloat16)
    d_gate = (dhid * up * sig * (1.0 + gate * (1.0 - sig))).astype(jnp.bfloat16)
    return (hidden, d_up, d_gate)


def contract_rows(left, right):
    return lax.dot_general(
        left, right, (((0,), (0,)), ((), ())), preferred_element_type=jnp.float32
    )


def on_device(inputs, grad_out, labels, w_gate, w_up, w_down):
    members = lax.axis_size("expert")
    replicas = lax.axis_size("dp")
    group = members // EXPERTS
    tok_count = inputs.shape[0]
    width = inputs.shape[1]
    columns = width // replicas
    capacity = 3 * tok_count // (2 * EXPERTS)
    label_col = labels[:, 0]
    onehot = (label_col[:, None] == jnp.arange(EXPERTS, dtype=jnp.int32)[None, :]).astype(jnp.int32)
    before = jnp.cumsum(onehot, axis=0) - onehot
    rank_in = jnp.sum(before * onehot, axis=1)
    slot_ids = label_col * capacity + rank_in

    both = jnp.stack([inputs, grad_out])
    slots = jnp.zeros((2, EXPERTS * capacity, width), jnp.bfloat16).at[:, slot_ids].set(both)
    send = slots.reshape(2, EXPERTS, capacity, replicas, columns)
    send = jnp.transpose(send, (3, 1, 0, 2, 4))
    send = jnp.broadcast_to(
        send[:, :, None], (replicas, EXPERTS, group, 2, capacity, columns)
    ).reshape(replicas * members, 2 * capacity * columns)
    recv = lax.all_to_all(send, ALL, 0, 0, tiled=True)
    recv = recv.reshape(replicas * members, 2, capacity, columns)
    rows_in = recv[:, 0].reshape(-1, columns)
    rows_grad = recv[:, 1].reshape(-1, columns)

    gate_part = jnp.dot(rows_in, w_gate, preferred_element_type=jnp.float32)
    up_part = jnp.dot(rows_in, w_up, preferred_element_type=jnp.float32)
    dhid_part = lax.dot_general(
        rows_grad, w_down, (((1,), (1,)), ((), ())), preferred_element_type=jnp.float32
    )
    parts = jnp.stack([gate_part, up_part, dhid_part]).astype(jnp.bfloat16)
    reduced = lax.psum_scatter(parts, "dp", scatter_dimension=2, tiled=True).astype(jnp.float32)
    hidden, d_up, d_gate = nonlinear(reduced[0], reduced[1], reduced[2])
    gathered = lax.all_gather(jnp.stack([hidden, d_up, d_gate]), "dp", axis=2, tiled=True)
    hidden, d_up, d_gate = gathered[0], gathered[1], gathered[2]

    d_rows = lax.dot_general(
        d_gate, w_gate, (((1,), (1,)), ((), ())), preferred_element_type=jnp.float32
    )
    d_rows = d_rows + lax.dot_general(
        d_up, w_up, (((1,), (1,)), ((), ())), preferred_element_type=jnp.float32
    )
    back = d_rows.astype(jnp.bfloat16).reshape(replicas * members, capacity * columns)
    back = lax.all_to_all(back, ALL, 0, 0, tiled=True)
    back = back.reshape(replicas, EXPERTS, group, capacity, columns).astype(jnp.float32)
    summed = jnp.sum(back, axis=2)
    summed = jnp.transpose(summed, (1, 2, 0, 3)).reshape(EXPERTS * capacity, width)
    grad_in = summed[slot_ids].astype(jnp.bfloat16)
    grad_gate = contract_rows(rows_in, d_gate).astype(jnp.bfloat16)
    grad_up = contract_rows(rows_in, d_up).astype(jnp.bfloat16)
    grad_down = contract_rows(hidden, rows_grad).astype(jnp.bfloat16)
    return (grad_in, grad_gate, grad_up, grad_down)


def solution(mesh):
    return jax.shard_map(
        on_device,
        mesh=mesh,
        in_specs=(
            P(ALL, None),
            P(ALL, None),
            P(ALL, None),
            P("dp", "expert"),
            P("dp", "expert"),
            P("expert", "dp"),
        ),
        out_specs=(
            P(ALL, None),
            P("dp", "expert"),
            P("dp", "expert"),
            P("expert", "dp"),
        ),
        check_vma=False,
    )
```

```python
import jax
import jax.numpy as jnp
from jax import lax
from jax.sharding import PartitionSpec as P

EXPERTS = 8
ALL = ("dp", "expert")


def nonlinear(gate, up, dhid):
    sig = jax.nn.sigmoid(gate)
    act = gate * sig
    hidden = (act * up).astype(jnp.bfloat16)
    d_up = (dhid * act).astype(jnp.bfloat16)
    d_gate = (dhid * up * sig * (1.0 + gate * (1.0 - sig))).astype(jnp.bfloat16)
    return (hidden, d_up, d_gate)


def contract_rows(left, right):
    return lax.dot_general(
        left, right, (((0,), (0,)), ((), ())), preferred_element_type=jnp.float32
    )


def scatter_partials(parts):
    replicas = lax.axis_size("dp")
    if replicas & (replicas - 1):
        return lax.psum_scatter(parts, "dp", scatter_dimension=parts.ndim - 1, tiled=True)
    index = lax.axis_index("dp")
    buf = parts
    dist = replicas // 2
    while dist >= 1:
        bit = (index // dist) % 2
        half = buf.shape[-1] // 2
        split = buf.reshape(buf.shape[:-1] + (2, half))
        keep = lax.dynamic_index_in_dim(split, bit, axis=split.ndim - 2, keepdims=False)
        give = lax.dynamic_index_in_dim(split, 1 - bit, axis=split.ndim - 2, keepdims=False)
        if dist == replicas // 2 and replicas > 2:
            give = give.astype(jnp.bfloat16)
        perm = [(j, j ^ dist) for j in range(replicas)]
        buf = keep + lax.ppermute(give, "dp", perm).astype(jnp.float32)
        dist //= 2
    return buf


def on_device(inputs, grad_out, labels, w_gate, w_up, w_down):
    members = lax.axis_size("expert")
    replicas = lax.axis_size("dp")
    group = members // EXPERTS
    tok_count = inputs.shape[0]
    width = inputs.shape[1]
    columns = width // replicas
    capacity = 3 * tok_count // (2 * EXPERTS)
    label_col = labels[:, 0]
    onehot = (label_col[:, None] == jnp.arange(EXPERTS, dtype=jnp.int32)[None, :]).astype(jnp.int32)
    before = jnp.cumsum(onehot, axis=0) - onehot
    rank_in = jnp.sum(before * onehot, axis=1)
    slot_ids = label_col * capacity + rank_in

    both = jnp.stack([inputs, grad_out])
    slots = jnp.zeros((2, EXPERTS * capacity, width), jnp.bfloat16).at[:, slot_ids].set(both)
    send = slots.reshape(2, EXPERTS, capacity, replicas, columns)
    send = jnp.transpose(send, (3, 1, 0, 2, 4))
    send = jnp.broadcast_to(
        send[:, :, None], (replicas, EXPERTS, group, 2, capacity, columns)
    ).reshape(replicas * members, 2 * capacity * columns)
    recv = lax.all_to_all(send, ALL, 0, 0, tiled=True)
    recv = recv.reshape(replicas * members, 2, capacity, columns)
    rows_in = recv[:, 0].reshape(-1, columns)
    rows_grad = recv[:, 1].reshape(-1, columns)

    gate_part = jnp.dot(rows_in, w_gate, preferred_element_type=jnp.float32)
    up_part = jnp.dot(rows_in, w_up, preferred_element_type=jnp.float32)
    dhid_part = lax.dot_general(
        rows_grad, w_down, (((1,), (1,)), ((), ())), preferred_element_type=jnp.float32
    )
    reduced = scatter_partials(jnp.stack([gate_part, up_part, dhid_part]))
    hidden, d_up, d_gate = nonlinear(reduced[0], reduced[1], reduced[2])
    gathered = lax.all_gather(jnp.stack([hidden, d_up, d_gate]), "dp", axis=2, tiled=True)
    hidden, d_up, d_gate = gathered[0], gathered[1], gathered[2]

    d_rows = lax.dot_general(
        d_gate, w_gate, (((1,), (1,)), ((), ())), preferred_element_type=jnp.float32
    )
    d_rows = d_rows + lax.dot_general(
        d_up, w_up, (((1,), (1,)), ((), ())), preferred_element_type=jnp.float32
    )
    back = d_rows.astype(jnp.bfloat16).reshape(replicas * members, capacity * columns)
    back = lax.all_to_all(back, ALL, 0, 0, tiled=True)
    back = back.reshape(replicas, EXPERTS, group, capacity, columns).astype(jnp.float32)
    summed = jnp.sum(back, axis=2)
    summed = jnp.transpose(summed, (1, 2, 0, 3)).reshape(EXPERTS * capacity, width)
    grad_in = summed[slot_ids].astype(jnp.bfloat16)
    grad_gate = contract_rows(rows_in, d_gate).astype(jnp.bfloat16)
    grad_up = contract_rows(rows_in, d_up).astype(jnp.bfloat16)
    grad_down = contract_rows(hidden, rows_grad).astype(jnp.bfloat16)
    return (grad_in, grad_gate, grad_up, grad_down)


def solution(mesh):
    return jax.shard_map(
        on_device,
        mesh=mesh,
        in_specs=(
            P(ALL, None),
            P(ALL, None),
            P(ALL, None),
            P("dp", "expert"),
            P("dp", "expert"),
            P("expert", "dp"),
        ),
        out_specs=(
            P(ALL, None),
            P("dp", "expert"),
            P("dp", "expert"),
            P("expert", "dp"),
        ),
        check_vma=False,
    )
```

```python
import jax
import jax.numpy as jnp
from jax import lax
from jax.sharding import PartitionSpec as P

EXPERTS = 8
ALL = ("dp", "expert")
CHUNKS = 2
LINK = jnp.float32


def nonlinear(gate, up, dhid):
    sig = jax.nn.sigmoid(gate)
    act = gate * sig
    hidden = (act * up).astype(jnp.bfloat16)
    d_up = (dhid * act).astype(jnp.bfloat16)
    d_gate = (dhid * up * sig * (1.0 + gate * (1.0 - sig))).astype(jnp.bfloat16)
    return (hidden, d_up, d_gate)


def contract_rows(left, right):
    return lax.dot_general(
        left, right, (((0,), (0,)), ((), ())), preferred_element_type=jnp.float32
    )


def on_device(inputs, grad_out, labels, w_gate, w_up, w_down):
    members = lax.axis_size("expert")
    replicas = lax.axis_size("dp")
    group = members // EXPERTS
    tok_count = inputs.shape[0]
    width = inputs.shape[1]
    columns = width // replicas
    capacity = 3 * tok_count // (2 * EXPERTS)
    label_col = labels[:, 0]
    onehot = (label_col[:, None] == jnp.arange(EXPERTS, dtype=jnp.int32)[None, :]).astype(jnp.int32)
    before = jnp.cumsum(onehot, axis=0) - onehot
    rank_in = jnp.sum(before * onehot, axis=1)
    slot_ids = label_col * capacity + rank_in

    both = jnp.stack([inputs, grad_out])
    slots = jnp.zeros((2, EXPERTS * capacity, width), jnp.bfloat16).at[:, slot_ids].set(both)
    send = slots.reshape(2, EXPERTS, capacity, replicas, columns)
    send = jnp.transpose(send, (3, 1, 0, 2, 4))
    send = jnp.broadcast_to(
        send[:, :, None], (replicas, EXPERTS, group, 2, capacity, columns)
    ).reshape(replicas * members, 2 * capacity * columns)
    recv = lax.all_to_all(send, ALL, 0, 0, tiled=True)
    recv = recv.reshape(replicas * members, 2, capacity, columns)
    rows_in = recv[:, 0].reshape(-1, columns)
    rows_grad = recv[:, 1].reshape(-1, columns)

    ff = w_gate.shape[1]
    step = ff // CHUNKS
    d_rows = None
    grads = ([], [], [])
    for k in range(CHUNKS):
        cols = slice(k * step, (k + 1) * step)
        g_mat, u_mat, d_mat = w_gate[:, cols], w_up[:, cols], w_down[cols, :]
        gate_part = jnp.dot(rows_in, g_mat, preferred_element_type=jnp.float32)
        up_part = jnp.dot(rows_in, u_mat, preferred_element_type=jnp.float32)
        dhid_part = lax.dot_general(
            rows_grad, d_mat, (((1,), (1,)), ((), ())), preferred_element_type=jnp.float32
        )
        parts = jnp.stack([gate_part, up_part, dhid_part]).astype(LINK)
        reduced = lax.psum_scatter(parts, "dp", scatter_dimension=2, tiled=True)
        reduced = reduced.astype(jnp.float32)
        hidden, d_up, d_gate = nonlinear(reduced[0], reduced[1], reduced[2])
        gathered = lax.all_gather(jnp.stack([hidden, d_up, d_gate]), "dp", axis=2, tiled=True)
        hidden, d_up, d_gate = gathered[0], gathered[1], gathered[2]
        part_rows = lax.dot_general(
            d_gate, g_mat, (((1,), (1,)), ((), ())), preferred_element_type=jnp.float32
        ) + lax.dot_general(
            d_up, u_mat, (((1,), (1,)), ((), ())), preferred_element_type=jnp.float32
        )
        d_rows = part_rows if d_rows is None else d_rows + part_rows
        grads[0].append(contract_rows(rows_in, d_gate).astype(jnp.bfloat16))
        grads[1].append(contract_rows(rows_in, d_up).astype(jnp.bfloat16))
        grads[2].append(contract_rows(hidden, rows_grad).astype(jnp.bfloat16))
    back = d_rows.astype(jnp.bfloat16).reshape(replicas * members, capacity * columns)
    back = lax.all_to_all(back, ALL, 0, 0, tiled=True)
    back = back.reshape(replicas, EXPERTS, group, capacity, columns).astype(jnp.float32)
    summed = jnp.sum(back, axis=2)
    summed = jnp.transpose(summed, (1, 2, 0, 3)).reshape(EXPERTS * capacity, width)
    grad_in = summed[slot_ids].astype(jnp.bfloat16)
    grad_gate = jnp.concatenate(grads[0], axis=1)
    grad_up = jnp.concatenate(grads[1], axis=1)
    grad_down = jnp.concatenate(grads[2], axis=0)
    return (grad_in, grad_gate, grad_up, grad_down)


def solution(mesh):
    return jax.shard_map(
        on_device,
        mesh=mesh,
        in_specs=(
            P(ALL, None),
            P(ALL, None),
            P(ALL, None),
            P("dp", "expert"),
            P("dp", "expert"),
            P("expert", "dp"),
        ),
        out_specs=(
            P(ALL, None),
            P("dp", "expert"),
            P("dp", "expert"),
            P("expert", "dp"),
        ),
        check_vma=False,
    )
```

```python
import jax
import jax.numpy as jnp
from jax import lax
from jax.sharding import PartitionSpec as P
from jax.experimental import pallas as pl
from jax.experimental.pallas import tpu as pltpu

EXPERTS = 8
ALL = ("dp", "expert")


def nonlinear(gate, up, dhid):
    sig = jax.nn.sigmoid(gate)
    act = gate * sig
    hidden = (act * up).astype(jnp.bfloat16)
    d_up = (dhid * act).astype(jnp.bfloat16)
    d_gate = (dhid * up * sig * (1.0 + gate * (1.0 - sig))).astype(jnp.bfloat16)
    return (hidden, d_up, d_gate)


def contract_rows(left, right):
    return lax.dot_general(
        left, right, (((0,), (0,)), ((), ())), preferred_element_type=jnp.float32
    )


def _bwd_body(dg_ref, du_ref, ht_ref, xt_ref, y_ref, wg_ref, wu_ref,
              drows_ref, gg_ref, gu_ref, gd_ref):
    @pl.when(pl.program_id(0) == 0)
    def _():
        drows_ref[...] = jnp.zeros_like(drows_ref)
    dg = dg_ref[...]
    du = du_ref[...]
    nt = (((1,), (1,)), ((), ()))
    drows_ref[...] += lax.dot_general(dg, wg_ref[...], nt, preferred_element_type=jnp.float32) + \
        lax.dot_general(du, wu_ref[...], nt, preferred_element_type=jnp.float32)
    xt = xt_ref[...]
    gg_ref[...] = jnp.dot(xt, dg, preferred_element_type=jnp.float32).astype(gg_ref.dtype)
    gu_ref[...] = jnp.dot(xt, du, preferred_element_type=jnp.float32).astype(gu_ref.dtype)
    gd_ref[...] = jnp.dot(ht_ref[...], y_ref[...], preferred_element_type=jnp.float32).astype(gd_ref.dtype)

def fused_backward(d_gate, d_up, hidden, rows_in, rows_grad, w_gate, w_up):
    rows, ff = d_gate.shape
    cols = rows_in.shape[1]
    tile = 512 if ff % 512 == 0 else ff
    steps = ff // tile
    hidden_t = hidden.T
    rows_in_t = rows_in.T
    bf = jnp.bfloat16
    return pl.pallas_call(
        _bwd_body,
        grid=(steps,),
        in_specs=[
            pl.BlockSpec((rows, tile), lambda k: (0, k)),
            pl.BlockSpec((rows, tile), lambda k: (0, k)),
            pl.BlockSpec((tile, rows), lambda k: (k, 0)),
            pl.BlockSpec((cols, rows), lambda k: (0, 0)),
            pl.BlockSpec((rows, cols), lambda k: (0, 0)),
            pl.BlockSpec((cols, tile), lambda k: (0, k)),
            pl.BlockSpec((cols, tile), lambda k: (0, k)),
        ],
        out_specs=[
            pl.BlockSpec((rows, cols), lambda k: (0, 0)),
            pl.BlockSpec((cols, tile), lambda k: (0, k)),
            pl.BlockSpec((cols, tile), lambda k: (0, k)),
            pl.BlockSpec((tile, cols), lambda k: (k, 0)),
        ],
        out_shape=[
            jax.ShapeDtypeStruct((rows, cols), jnp.float32),
            jax.ShapeDtypeStruct((cols, ff), bf),
            jax.ShapeDtypeStruct((cols, ff), bf),
            jax.ShapeDtypeStruct((ff, cols), bf),
        ],
        compiler_params=pltpu.CompilerParams(dimension_semantics=("arbitrary",)),
        cost_estimate=pl.CostEstimate(
            flops=2 * rows * ff * cols * 5, transcendentals=0,
            bytes_accessed=2 * (2 * cols * ff + 3 * cols * ff + 3 * rows * ff)),
    )(d_gate, d_up, hidden_t, rows_in_t, rows_grad, w_gate, w_up)


def on_device(inputs, grad_out, labels, w_gate, w_up, w_down):
    members = lax.axis_size("expert")
    replicas = lax.axis_size("dp")
    group = members // EXPERTS
    tok_count = inputs.shape[0]
    width = inputs.shape[1]
    columns = width // replicas
    capacity = 3 * tok_count // (2 * EXPERTS)
    label_col = labels[:, 0]
    onehot = (label_col[:, None] == jnp.arange(EXPERTS, dtype=jnp.int32)[None, :]).astype(jnp.int32)
    before = jnp.cumsum(onehot, axis=0) - onehot
    rank_in = jnp.sum(before * onehot, axis=1)
    slot_ids = label_col * capacity + rank_in

    both = jnp.stack([inputs, grad_out])
    slots = jnp.zeros((2, EXPERTS * capacity, width), jnp.bfloat16).at[:, slot_ids].set(both)
    send = slots.reshape(2, EXPERTS, capacity, replicas, columns)
    send = jnp.transpose(send, (3, 1, 0, 2, 4))
    send = jnp.broadcast_to(
        send[:, :, None], (replicas, EXPERTS, group, 2, capacity, columns)
    ).reshape(replicas * members, 2 * capacity * columns)
    recv = lax.all_to_all(send, ALL, 0, 0, tiled=True)
    recv = recv.reshape(replicas * members, 2, capacity, columns)
    rows_in = recv[:, 0].reshape(-1, columns)
    rows_grad = recv[:, 1].reshape(-1, columns)

    gate_part = jnp.dot(rows_in, w_gate, preferred_element_type=jnp.float32)
    up_part = jnp.dot(rows_in, w_up, preferred_element_type=jnp.float32)
    dhid_part = lax.dot_general(
        rows_grad, w_down, (((1,), (1,)), ((), ())), preferred_element_type=jnp.float32
    )
    parts = jnp.stack([gate_part, up_part, dhid_part]).astype(jnp.bfloat16)
    reduced = lax.psum_scatter(parts, "dp", scatter_dimension=2, tiled=True).astype(jnp.float32)
    hidden, d_up, d_gate = nonlinear(reduced[0], reduced[1], reduced[2])
    gathered = lax.all_gather(jnp.stack([hidden, d_up, d_gate]), "dp", axis=2, tiled=True)
    hidden, d_up, d_gate = gathered[0], gathered[1], gathered[2]

    d_rows, grad_gate, grad_up, grad_down = fused_backward(
        d_gate, d_up, hidden, rows_in, rows_grad, w_gate, w_up
    )
    back = d_rows.astype(jnp.bfloat16).reshape(replicas * members, capacity * columns)
    back = lax.all_to_all(back, ALL, 0, 0, tiled=True)
    back = back.reshape(replicas, EXPERTS, group, capacity, columns).astype(jnp.float32)
    summed = jnp.sum(back, axis=2)
    summed = jnp.transpose(summed, (1, 2, 0, 3)).reshape(EXPERTS * capacity, width)
    grad_in = summed[slot_ids].astype(jnp.bfloat16)
    return (grad_in, grad_gate, grad_up, grad_down)


def solution(mesh):
    return jax.shard_map(
        on_device,
        mesh=mesh,
        in_specs=(
            P(ALL, None),
            P(ALL, None),
            P(ALL, None),
            P("dp", "expert"),
            P("dp", "expert"),
            P("expert", "dp"),
        ),
        out_specs=(
            P(ALL, None),
            P("dp", "expert"),
            P("dp", "expert"),
            P("expert", "dp"),
        ),
        check_vma=False,
    )
```

```python
import jax
import jax.numpy as jnp
from jax import lax
from jax.sharding import PartitionSpec as P
from jax.experimental import pallas as pl
from jax.experimental.pallas import tpu as pltpu

EXPERTS = 8
ALL = ("dp", "expert")


def nonlinear(gate, up, dhid):
    sig = jax.nn.sigmoid(gate)
    act = gate * sig
    hidden = (act * up).astype(jnp.bfloat16)
    d_up = (dhid * act).astype(jnp.bfloat16)
    d_gate = (dhid * up * sig * (1.0 + gate * (1.0 - sig))).astype(jnp.bfloat16)
    return (hidden, d_up, d_gate)


def contract_rows(left, right):
    return lax.dot_general(
        left, right, (((0,), (0,)), ((), ())), preferred_element_type=jnp.float32
    )


def _bwd_body(dg_ref, du_ref, h_ref, x_ref, y_ref, wg_ref, wu_ref,
              drows_ref, gg_ref, gu_ref, gd_ref):
    @pl.when(pl.program_id(0) == 0)
    def _():
        drows_ref[...] = jnp.zeros_like(drows_ref)
    dg = dg_ref[...]
    du = du_ref[...]
    nt = (((1,), (1,)), ((), ()))
    tn = (((0,), (0,)), ((), ()))
    drows_ref[...] += lax.dot_general(dg, wg_ref[...], nt, preferred_element_type=jnp.float32) + \
        lax.dot_general(du, wu_ref[...], nt, preferred_element_type=jnp.float32)
    x = x_ref[...]
    gg_ref[...] = lax.dot_general(x, dg, tn, preferred_element_type=jnp.float32).astype(gg_ref.dtype)
    gu_ref[...] = lax.dot_general(x, du, tn, preferred_element_type=jnp.float32).astype(gu_ref.dtype)
    gd_ref[...] = lax.dot_general(h_ref[...], y_ref[...], tn, preferred_element_type=jnp.float32).astype(gd_ref.dtype)


def fused_backward(gathered, rows_in, rows_grad, w_gate, w_up, interpret=False):
    rows, ff = gathered.shape[1], gathered.shape[2]
    cols = rows_in.shape[1]
    tile = 512 if ff % 512 == 0 else ff
    steps = ff // tile
    bf = jnp.bfloat16

    def plane(p):
        return pl.BlockSpec((None, rows, tile), lambda k: (p, 0, k))

    return pl.pallas_call(
        _bwd_body,
        grid=(steps,),
        in_specs=[
            plane(2),
            plane(1),
            plane(0),
            pl.BlockSpec((rows, cols), lambda k: (0, 0)),
            pl.BlockSpec((rows, cols), lambda k: (0, 0)),
            pl.BlockSpec((cols, tile), lambda k: (0, k)),
            pl.BlockSpec((cols, tile), lambda k: (0, k)),
        ],
        out_specs=[
            pl.BlockSpec((rows, cols), lambda k: (0, 0)),
            pl.BlockSpec((cols, tile), lambda k: (0, k)),
            pl.BlockSpec((cols, tile), lambda k: (0, k)),
            pl.BlockSpec((tile, cols), lambda k: (k, 0)),
        ],
        out_shape=[
            jax.ShapeDtypeStruct((rows, cols), jnp.float32),
            jax.ShapeDtypeStruct((cols, ff), bf),
            jax.ShapeDtypeStruct((cols, ff), bf),
            jax.ShapeDtypeStruct((ff, cols), bf),
        ],
        compiler_params=pltpu.CompilerParams(dimension_semantics=("arbitrary",)),
        cost_estimate=pl.CostEstimate(
            flops=2 * rows * ff * cols * 5, transcendentals=0,
            bytes_accessed=2 * (2 * cols * ff + 3 * cols * ff + 3 * rows * ff)),
        interpret=interpret,
    )(gathered, gathered, gathered, rows_in, rows_grad, w_gate, w_up)


def on_device(inputs, grad_out, labels, w_gate, w_up, w_down):
    members = lax.axis_size("expert")
    replicas = lax.axis_size("dp")
    group = members // EXPERTS
    tok_count = inputs.shape[0]
    width = inputs.shape[1]
    columns = width // replicas
    capacity = 3 * tok_count // (2 * EXPERTS)
    label_col = labels[:, 0]
    onehot = (label_col[:, None] == jnp.arange(EXPERTS, dtype=jnp.int32)[None, :]).astype(jnp.int32)
    before = jnp.cumsum(onehot, axis=0) - onehot
    rank_in = jnp.sum(before * onehot, axis=1)
    slot_ids = label_col * capacity + rank_in

    both = jnp.stack([inputs, grad_out])
    slots = jnp.zeros((2, EXPERTS * capacity, width), jnp.bfloat16).at[:, slot_ids].set(both)
    send = slots.reshape(2, EXPERTS, capacity, replicas, columns)
    send = jnp.transpose(send, (3, 1, 0, 2, 4))
    send = jnp.broadcast_to(
        send[:, :, None], (replicas, EXPERTS, group, 2, capacity, columns)
    ).reshape(replicas * members, 2 * capacity * columns)
    recv = lax.all_to_all(send, ALL, 0, 0, tiled=True)
    recv = recv.reshape(replicas * members, 2, capacity, columns)
    rows_in = recv[:, 0].reshape(-1, columns)
    rows_grad = recv[:, 1].reshape(-1, columns)

    gate_part = jnp.dot(rows_in, w_gate, preferred_element_type=jnp.float32)
    up_part = jnp.dot(rows_in, w_up, preferred_element_type=jnp.float32)
    dhid_part = lax.dot_general(
        rows_grad, w_down, (((1,), (1,)), ((), ())), preferred_element_type=jnp.float32
    )
    parts = jnp.stack([gate_part, up_part, dhid_part]).astype(jnp.bfloat16)
    reduced = lax.psum_scatter(parts, "dp", scatter_dimension=2, tiled=True).astype(jnp.float32)
    hidden, d_up, d_gate = nonlinear(reduced[0], reduced[1], reduced[2])
    gathered = lax.all_gather(jnp.stack([hidden, d_up, d_gate]), "dp", axis=2, tiled=True)

    d_rows, grad_gate, grad_up, grad_down = fused_backward(
        gathered, rows_in, rows_grad, w_gate, w_up
    )
    back = d_rows.astype(jnp.bfloat16).reshape(replicas * members, capacity * columns)
    back = lax.all_to_all(back, ALL, 0, 0, tiled=True)
    back = back.reshape(replicas, EXPERTS, group, capacity, columns).astype(jnp.float32)
    summed = jnp.sum(back, axis=2)
    summed = jnp.transpose(summed, (1, 2, 0, 3)).reshape(EXPERTS * capacity, width)
    grad_in = summed[slot_ids].astype(jnp.bfloat16)
    return (grad_in, grad_gate, grad_up, grad_down)


def solution(mesh):
    return jax.shard_map(
        on_device,
        mesh=mesh,
        in_specs=(
            P(ALL, None),
            P(ALL, None),
            P(ALL, None),
            P("dp", "expert"),
            P("dp", "expert"),
            P("expert", "dp"),
        ),
        out_specs=(
            P(ALL, None),
            P("dp", "expert"),
            P("dp", "expert"),
            P("expert", "dp"),
        ),
        check_vma=False,
    )
```

```python
import jax
import jax.numpy as jnp
from jax import lax
from jax.sharding import PartitionSpec as P
from jax.experimental import pallas as pl
from jax.experimental.pallas import tpu as pltpu

EXPERTS = 8
ALL = ("dp", "expert")


def nonlinear(gate, up, dhid):
    sig = jax.nn.sigmoid(gate)
    act = gate * sig
    hidden = (act * up).astype(jnp.bfloat16)
    d_up = (dhid * act).astype(jnp.bfloat16)
    d_gate = (dhid * up * sig * (1.0 + gate * (1.0 - sig))).astype(jnp.bfloat16)
    return (hidden, d_up, d_gate)


def contract_rows(left, right):
    return lax.dot_general(
        left, right, (((0,), (0,)), ((), ())), preferred_element_type=jnp.float32
    )


def _rows_body(dg_ref, du_ref, wg_ref, wu_ref, drows_ref):
    @pl.when(pl.program_id(0) == 0)
    def _():
        drows_ref[...] = jnp.zeros_like(drows_ref)
    nt = (((1,), (1,)), ((), ()))
    drows_ref[...] += lax.dot_general(
        dg_ref[...], wg_ref[...], nt, preferred_element_type=jnp.float32
    ) + lax.dot_general(du_ref[...], wu_ref[...], nt, preferred_element_type=jnp.float32)


def _grads_body(dg_ref, du_ref, h_ref, x_ref, y_ref, gg_ref, gu_ref, gd_ref):
    tn = (((0,), (0,)), ((), ()))
    x = x_ref[...]
    gg_ref[...] = lax.dot_general(x, dg_ref[...], tn, preferred_element_type=jnp.float32).astype(gg_ref.dtype)
    gu_ref[...] = lax.dot_general(x, du_ref[...], tn, preferred_element_type=jnp.float32).astype(gu_ref.dtype)
    gd_ref[...] = lax.dot_general(h_ref[...], y_ref[...], tn, preferred_element_type=jnp.float32).astype(gd_ref.dtype)


def backward_rows(gathered, w_gate, w_up):
    rows, ff = gathered.shape[1], gathered.shape[2]
    cols = w_gate.shape[0]
    tile = 512 if ff % 512 == 0 else ff

    def plane(p):
        return pl.BlockSpec((None, rows, tile), lambda k: (p, 0, k))

    return pl.pallas_call(
        _rows_body,
        grid=(ff // tile,),
        in_specs=[
            plane(2),
            plane(1),
            pl.BlockSpec((cols, tile), lambda k: (0, k)),
            pl.BlockSpec((cols, tile), lambda k: (0, k)),
        ],
        out_specs=pl.BlockSpec((rows, cols), lambda k: (0, 0)),
        out_shape=jax.ShapeDtypeStruct((rows, cols), jnp.float32),
        compiler_params=pltpu.CompilerParams(dimension_semantics=("arbitrary",)),
        cost_estimate=pl.CostEstimate(
            flops=4 * rows * ff * cols, transcendentals=0,
            bytes_accessed=2 * (2 * cols * ff + 2 * rows * ff) + 4 * rows * cols),
    )(gathered, gathered, w_gate, w_up)


def backward_grads(gathered, rows_in, rows_grad):
    rows, ff = gathered.shape[1], gathered.shape[2]
    cols = rows_in.shape[1]
    tile = 512 if ff % 512 == 0 else ff
    bf = jnp.bfloat16

    def plane(p):
        return pl.BlockSpec((None, rows, tile), lambda k: (p, 0, k))

    return pl.pallas_call(
        _grads_body,
        grid=(ff // tile,),
        in_specs=[
            plane(2),
            plane(1),
            plane(0),
            pl.BlockSpec((rows, cols), lambda k: (0, 0)),
            pl.BlockSpec((rows, cols), lambda k: (0, 0)),
        ],
        out_specs=[
            pl.BlockSpec((cols, tile), lambda k: (0, k)),
            pl.BlockSpec((cols, tile), lambda k: (0, k)),
            pl.BlockSpec((tile, cols), lambda k: (k, 0)),
        ],
        out_shape=[
            jax.ShapeDtypeStruct((cols, ff), bf),
            jax.ShapeDtypeStruct((cols, ff), bf),
            jax.ShapeDtypeStruct((ff, cols), bf),
        ],
        compiler_params=pltpu.CompilerParams(dimension_semantics=("parallel",)),
        cost_estimate=pl.CostEstimate(
            flops=6 * rows * ff * cols, transcendentals=0,
            bytes_accessed=2 * (3 * cols * ff + 3 * rows * ff + 2 * rows * cols)),
    )(gathered, gathered, gathered, rows_in, rows_grad)


def on_device(inputs, grad_out, labels, w_gate, w_up, w_down):
    members = lax.axis_size("expert")
    replicas = lax.axis_size("dp")
    group = members // EXPERTS
    tok_count = inputs.shape[0]
    width = inputs.shape[1]
    columns = width // replicas
    capacity = 3 * tok_count // (2 * EXPERTS)
    label_col = labels[:, 0]
    onehot = (label_col[:, None] == jnp.arange(EXPERTS, dtype=jnp.int32)[None, :]).astype(jnp.int32)
    before = jnp.cumsum(onehot, axis=0) - onehot
    rank_in = jnp.sum(before * onehot, axis=1)
    slot_ids = label_col * capacity + rank_in

    both = jnp.stack([inputs, grad_out])
    slots = jnp.zeros((2, EXPERTS * capacity, width), jnp.bfloat16).at[:, slot_ids].set(both)
    send = slots.reshape(2, EXPERTS, capacity, replicas, columns)
    send = jnp.transpose(send, (3, 1, 0, 2, 4))
    send = jnp.broadcast_to(
        send[:, :, None], (replicas, EXPERTS, group, 2, capacity, columns)
    ).reshape(replicas * members, 2 * capacity * columns)
    recv = lax.all_to_all(send, ALL, 0, 0, tiled=True)
    recv = recv.reshape(replicas * members, 2, capacity, columns)
    rows_in = recv[:, 0].reshape(-1, columns)
    rows_grad = recv[:, 1].reshape(-1, columns)

    gate_part = jnp.dot(rows_in, w_gate, preferred_element_type=jnp.float32)
    up_part = jnp.dot(rows_in, w_up, preferred_element_type=jnp.float32)
    dhid_part = lax.dot_general(
        rows_grad, w_down, (((1,), (1,)), ((), ())), preferred_element_type=jnp.float32
    )
    parts = jnp.stack([gate_part, up_part, dhid_part]).astype(jnp.bfloat16)
    reduced = lax.psum_scatter(parts, "dp", scatter_dimension=2, tiled=True).astype(jnp.float32)
    hidden, d_up, d_gate = nonlinear(reduced[0], reduced[1], reduced[2])
    gathered = lax.all_gather(jnp.stack([hidden, d_up, d_gate]), "dp", axis=2, tiled=True)

    d_rows = backward_rows(gathered, w_gate, w_up)
    back = d_rows.astype(jnp.bfloat16).reshape(replicas * members, capacity * columns)
    back = lax.all_to_all(back, ALL, 0, 0, tiled=True)
    back = back.reshape(replicas, EXPERTS, group, capacity, columns).astype(jnp.float32)
    summed = jnp.sum(back, axis=2)
    summed = jnp.transpose(summed, (1, 2, 0, 3)).reshape(EXPERTS * capacity, width)
    grad_in = summed[slot_ids].astype(jnp.bfloat16)
    grad_gate, grad_up, grad_down = backward_grads(gathered, rows_in, rows_grad)
    return (grad_in, grad_gate, grad_up, grad_down)


def solution(mesh):
    return jax.shard_map(
        on_device,
        mesh=mesh,
        in_specs=(
            P(ALL, None),
            P(ALL, None),
            P(ALL, None),
            P("dp", "expert"),
            P("dp", "expert"),
            P("expert", "dp"),
        ),
        out_specs=(
            P(ALL, None),
            P("dp", "expert"),
            P("dp", "expert"),
            P("expert", "dp"),
        ),
        check_vma=False,
    )
```

```python
import jax
import jax.numpy as jnp
from jax import lax
from jax.sharding import PartitionSpec as P
from jax.experimental import pallas as pl
from jax.experimental.pallas import tpu as pltpu

EXPERTS = 8
ALL = ("dp", "expert")


def nonlinear(gate, up, dhid):
    sig = jax.nn.sigmoid(gate)
    act = gate * sig
    hidden = (act * up).astype(jnp.bfloat16)
    d_up = (dhid * act).astype(jnp.bfloat16)
    d_gate = (dhid * up * sig * (1.0 + gate * (1.0 - sig))).astype(jnp.bfloat16)
    return (hidden, d_up, d_gate)


def contract_rows(left, right):
    return lax.dot_general(
        left, right, (((0,), (0,)), ((), ())), preferred_element_type=jnp.float32
    )


def _rows_body(dg_ref, du_ref, wg_ref, wu_ref, drows_ref):
    @pl.when(pl.program_id(0) == 0)
    def _():
        drows_ref[...] = jnp.zeros_like(drows_ref)
    nt = (((1,), (1,)), ((), ()))
    drows_ref[...] += lax.dot_general(
        wg_ref[...], dg_ref[...], nt, preferred_element_type=jnp.float32
    ) + lax.dot_general(wu_ref[...], du_ref[...], nt, preferred_element_type=jnp.float32)


def _grads_body(dg_ref, du_ref, h_ref, x_ref, y_ref, gg_ref, gu_ref, gd_ref):
    tn = (((0,), (0,)), ((), ()))
    x = x_ref[...]
    gg_ref[...] = lax.dot_general(x, dg_ref[...], tn, preferred_element_type=jnp.float32).astype(gg_ref.dtype)
    gu_ref[...] = lax.dot_general(x, du_ref[...], tn, preferred_element_type=jnp.float32).astype(gu_ref.dtype)
    gd_ref[...] = lax.dot_general(h_ref[...], y_ref[...], tn, preferred_element_type=jnp.float32).astype(gd_ref.dtype)


def backward_rows(gathered, w_gate, w_up):
    rows, ff = gathered.shape[1], gathered.shape[2]
    cols = w_gate.shape[0]
    tile = 512 if ff % 512 == 0 else ff

    def plane(p):
        return pl.BlockSpec((None, rows, tile), lambda k: (p, 0, k))

    return pl.pallas_call(
        _rows_body,
        grid=(ff // tile,),
        in_specs=[
            plane(2),
            plane(1),
            pl.BlockSpec((cols, tile), lambda k: (0, k)),
            pl.BlockSpec((cols, tile), lambda k: (0, k)),
        ],
        out_specs=pl.BlockSpec((cols, rows), lambda k: (0, 0)),
        out_shape=jax.ShapeDtypeStruct((cols, rows), jnp.float32),
        compiler_params=pltpu.CompilerParams(dimension_semantics=("arbitrary",)),
        cost_estimate=pl.CostEstimate(
            flops=4 * rows * ff * cols, transcendentals=0,
            bytes_accessed=2 * (2 * cols * ff + 2 * rows * ff) + 4 * rows * cols),
    )(gathered, gathered, w_gate, w_up)


def backward_grads(gathered, rows_in, rows_grad):
    rows, ff = gathered.shape[1], gathered.shape[2]
    cols = rows_in.shape[1]
    tile = 512 if ff % 512 == 0 else ff
    bf = jnp.bfloat16

    def plane(p):
        return pl.BlockSpec((None, rows, tile), lambda k: (p, 0, k))

    return pl.pallas_call(
        _grads_body,
        grid=(ff // tile,),
        in_specs=[
            plane(2),
            plane(1),
            plane(0),
            pl.BlockSpec((rows, cols), lambda k: (0, 0)),
            pl.BlockSpec((rows, cols), lambda k: (0, 0)),
        ],
        out_specs=[
            pl.BlockSpec((cols, tile), lambda k: (0, k)),
            pl.BlockSpec((cols, tile), lambda k: (0, k)),
            pl.BlockSpec((tile, cols), lambda k: (k, 0)),
        ],
        out_shape=[
            jax.ShapeDtypeStruct((cols, ff), bf),
            jax.ShapeDtypeStruct((cols, ff), bf),
            jax.ShapeDtypeStruct((ff, cols), bf),
        ],
        compiler_params=pltpu.CompilerParams(dimension_semantics=("parallel",)),
        cost_estimate=pl.CostEstimate(
            flops=6 * rows * ff * cols, transcendentals=0,
            bytes_accessed=2 * (3 * cols * ff + 3 * rows * ff + 2 * rows * cols)),
    )(gathered, gathered, gathered, rows_in, rows_grad)


def on_device(inputs, grad_out, labels, w_gate, w_up, w_down):
    members = lax.axis_size("expert")
    replicas = lax.axis_size("dp")
    group = members // EXPERTS
    tok_count = inputs.shape[0]
    width = inputs.shape[1]
    columns = width // replicas
    capacity = 3 * tok_count // (2 * EXPERTS)
    label_col = labels[:, 0]
    onehot = (label_col[:, None] == jnp.arange(EXPERTS, dtype=jnp.int32)[None, :]).astype(jnp.int32)
    before = jnp.cumsum(onehot, axis=0) - onehot
    rank_in = jnp.sum(before * onehot, axis=1)
    slot_ids = label_col * capacity + rank_in

    both = jnp.stack([inputs, grad_out])
    slots = jnp.zeros((2, EXPERTS * capacity, width), jnp.bfloat16).at[:, slot_ids].set(both)
    send = slots.reshape(2, EXPERTS, capacity, replicas, columns)
    send = jnp.transpose(send, (3, 1, 0, 2, 4))
    send = jnp.broadcast_to(
        send[:, :, None], (replicas, EXPERTS, group, 2, capacity, columns)
    ).reshape(replicas * members, 2 * capacity * columns)
    recv = lax.all_to_all(send, ALL, 0, 0, tiled=True)
    recv = recv.reshape(replicas * members, 2, capacity, columns)
    rows_in = recv[:, 0].reshape(-1, columns)
    rows_grad = recv[:, 1].reshape(-1, columns)

    gate_part = jnp.dot(rows_in, w_gate, preferred_element_type=jnp.float32)
    up_part = jnp.dot(rows_in, w_up, preferred_element_type=jnp.float32)
    dhid_part = lax.dot_general(
        rows_grad, w_down, (((1,), (1,)), ((), ())), preferred_element_type=jnp.float32
    )
    parts = jnp.stack([gate_part, up_part, dhid_part]).astype(jnp.bfloat16)
    reduced = lax.psum_scatter(parts, "dp", scatter_dimension=2, tiled=True).astype(jnp.float32)
    hidden, d_up, d_gate = nonlinear(reduced[0], reduced[1], reduced[2])
    gathered = lax.all_gather(jnp.stack([hidden, d_up, d_gate]), "dp", axis=2, tiled=True)

    d_rows = backward_rows(gathered, w_gate, w_up).T
    back = d_rows.astype(jnp.bfloat16).reshape(replicas * members, capacity * columns)
    back = lax.all_to_all(back, ALL, 0, 0, tiled=True)
    back = back.reshape(replicas, EXPERTS, group, capacity, columns).astype(jnp.float32)
    summed = jnp.sum(back, axis=2)
    summed = jnp.transpose(summed, (1, 2, 0, 3)).reshape(EXPERTS * capacity, width)
    grad_in = summed[slot_ids].astype(jnp.bfloat16)
    grad_gate, grad_up, grad_down = backward_grads(gathered, rows_in, rows_grad)
    return (grad_in, grad_gate, grad_up, grad_down)


def solution(mesh):
    return jax.shard_map(
        on_device,
        mesh=mesh,
        in_specs=(
            P(ALL, None),
            P(ALL, None),
            P(ALL, None),
            P("dp", "expert"),
            P("dp", "expert"),
            P("expert", "dp"),
        ),
        out_specs=(
            P(ALL, None),
            P("dp", "expert"),
            P("dp", "expert"),
            P("expert", "dp"),
        ),
        check_vma=False,
    )
```

```python
import jax
import jax.numpy as jnp
from jax import lax
from jax.sharding import PartitionSpec as P
from jax.experimental import pallas as pl
from jax.experimental.pallas import tpu as pltpu

EXPERTS = 8
ALL = ("dp", "expert")


def nonlinear(gate, up, dhid):
    sig = jax.nn.sigmoid(gate)
    act = gate * sig
    hidden = (act * up).astype(jnp.bfloat16)
    d_up = (dhid * act).astype(jnp.bfloat16)
    d_gate = (dhid * up * sig * (1.0 + gate * (1.0 - sig))).astype(jnp.bfloat16)
    return (hidden, d_up, d_gate)


def contract_rows(left, right):
    return lax.dot_general(
        left, right, (((0,), (0,)), ((), ())), preferred_element_type=jnp.float32
    )


def _rows_body(dg_ref, du_ref, wg_ref, wu_ref, drows_ref):
    @pl.when(pl.program_id(0) == 0)
    def _():
        drows_ref[...] = jnp.zeros_like(drows_ref)
    nt = (((1,), (1,)), ((), ()))
    drows_ref[...] += lax.dot_general(
        wg_ref[...], dg_ref[...], nt, preferred_element_type=jnp.float32
    ) + lax.dot_general(wu_ref[...], du_ref[...], nt, preferred_element_type=jnp.float32)


def _grads_body(dg_ref, du_ref, h_ref, x_ref, y_ref, gg_ref, gu_ref, gd_ref):
    tn = (((0,), (0,)), ((), ()))
    x = x_ref[...]
    gg_ref[...] = lax.dot_general(x, dg_ref[...], tn, preferred_element_type=jnp.float32).astype(gg_ref.dtype)
    gu_ref[...] = lax.dot_general(x, du_ref[...], tn, preferred_element_type=jnp.float32).astype(gu_ref.dtype)
    gd_ref[...] = lax.dot_general(h_ref[...], y_ref[...], tn, preferred_element_type=jnp.float32).astype(gd_ref.dtype)


def backward_rows(gathered, w_gate, w_up):
    rows, ff = gathered.shape[1], gathered.shape[2]
    cols = w_gate.shape[0]
    tile = 1024 if ff % 1024 == 0 else ff

    def plane(p):
        return pl.BlockSpec((None, rows, tile), lambda k: (p, 0, k))

    return pl.pallas_call(
        _rows_body,
        grid=(ff // tile,),
        in_specs=[
            plane(2),
            plane(1),
            pl.BlockSpec((cols, tile), lambda k: (0, k)),
            pl.BlockSpec((cols, tile), lambda k: (0, k)),
        ],
        out_specs=pl.BlockSpec((cols, rows), lambda k: (0, 0)),
        out_shape=jax.ShapeDtypeStruct((cols, rows), jnp.float32),
        compiler_params=pltpu.CompilerParams(dimension_semantics=("arbitrary",)),
        cost_estimate=pl.CostEstimate(
            flops=4 * rows * ff * cols, transcendentals=0,
            bytes_accessed=2 * (2 * cols * ff + 2 * rows * ff) + 4 * rows * cols),
    )(gathered, gathered, w_gate, w_up)


def backward_grads(gathered, rows_in, rows_grad):
    rows, ff = gathered.shape[1], gathered.shape[2]
    cols = rows_in.shape[1]
    tile = 512 if ff % 512 == 0 else ff
    bf = jnp.bfloat16

    def plane(p):
        return pl.BlockSpec((None, rows, tile), lambda k: (p, 0, k))

    return pl.pallas_call(
        _grads_body,
        grid=(ff // tile,),
        in_specs=[
            plane(2),
            plane(1),
            plane(0),
            pl.BlockSpec((rows, cols), lambda k: (0, 0)),
            pl.BlockSpec((rows, cols), lambda k: (0, 0)),
        ],
        out_specs=[
            pl.BlockSpec((cols, tile), lambda k: (0, k)),
            pl.BlockSpec((cols, tile), lambda k: (0, k)),
            pl.BlockSpec((tile, cols), lambda k: (k, 0)),
        ],
        out_shape=[
            jax.ShapeDtypeStruct((cols, ff), bf),
            jax.ShapeDtypeStruct((cols, ff), bf),
            jax.ShapeDtypeStruct((ff, cols), bf),
        ],
        compiler_params=pltpu.CompilerParams(dimension_semantics=("parallel",)),
        cost_estimate=pl.CostEstimate(
            flops=6 * rows * ff * cols, transcendentals=0,
            bytes_accessed=2 * (3 * cols * ff + 3 * rows * ff + 2 * rows * cols)),
    )(gathered, gathered, gathered, rows_in, rows_grad)


def on_device(inputs, grad_out, labels, w_gate, w_up, w_down):
    members = lax.axis_size("expert")
    replicas = lax.axis_size("dp")
    group = members // EXPERTS
    tok_count = inputs.shape[0]
    width = inputs.shape[1]
    columns = width // replicas
    capacity = 3 * tok_count // (2 * EXPERTS)
    label_col = labels[:, 0]
    onehot = (label_col[:, None] == jnp.arange(EXPERTS, dtype=jnp.int32)[None, :]).astype(jnp.int32)
    before = jnp.cumsum(onehot, axis=0) - onehot
    rank_in = jnp.sum(before * onehot, axis=1)
    slot_ids = label_col * capacity + rank_in

    both = jnp.stack([inputs, grad_out])
    slots = jnp.zeros((2, EXPERTS * capacity, width), jnp.bfloat16).at[:, slot_ids].set(both)
    send = slots.reshape(2, EXPERTS, capacity, replicas, columns)
    send = jnp.transpose(send, (3, 1, 0, 2, 4))
    send = jnp.broadcast_to(
        send[:, :, None], (replicas, EXPERTS, group, 2, capacity, columns)
    ).reshape(replicas * members, 2 * capacity * columns)
    recv = lax.all_to_all(send, ALL, 0, 0, tiled=True)
    recv = recv.reshape(replicas * members, 2, capacity, columns)
    rows_in = recv[:, 0].reshape(-1, columns)
    rows_grad = recv[:, 1].reshape(-1, columns)

    gate_part = jnp.dot(rows_in, w_gate, preferred_element_type=jnp.float32)
    up_part = jnp.dot(rows_in, w_up, preferred_element_type=jnp.float32)
    dhid_part = lax.dot_general(
        rows_grad, w_down, (((1,), (1,)), ((), ())), preferred_element_type=jnp.float32
    )
    parts = jnp.stack([gate_part, up_part, dhid_part]).astype(jnp.bfloat16)
    reduced = lax.psum_scatter(parts, "dp", scatter_dimension=2, tiled=True).astype(jnp.float32)
    hidden, d_up, d_gate = nonlinear(reduced[0], reduced[1], reduced[2])
    gathered = lax.all_gather(jnp.stack([hidden, d_up, d_gate]), "dp", axis=2, tiled=True)

    d_rows = backward_rows(gathered, w_gate, w_up).T
    back = d_rows.astype(jnp.bfloat16).reshape(replicas * members, capacity * columns)
    back = lax.all_to_all(back, ALL, 0, 0, tiled=True)
    back = back.reshape(replicas, EXPERTS, group, capacity, columns).astype(jnp.float32)
    summed = jnp.sum(back, axis=2)
    summed = jnp.transpose(summed, (1, 2, 0, 3)).reshape(EXPERTS * capacity, width)
    grad_in = summed[slot_ids].astype(jnp.bfloat16)
    grad_gate, grad_up, grad_down = backward_grads(gathered, rows_in, rows_grad)
    return (grad_in, grad_gate, grad_up, grad_down)


def solution(mesh):
    return jax.shard_map(
        on_device,
        mesh=mesh,
        in_specs=(
            P(ALL, None),
            P(ALL, None),
            P(ALL, None),
            P("dp", "expert"),
            P("dp", "expert"),
            P("expert", "dp"),
        ),
        out_specs=(
            P(ALL, None),
            P("dp", "expert"),
            P("dp", "expert"),
            P("expert", "dp"),
        ),
        check_vma=False,
    )
```

```python
import jax
import jax.numpy as jnp
from jax import lax
from jax.sharding import PartitionSpec as P
from jax.experimental import pallas as pl
from jax.experimental.pallas import tpu as pltpu

EXPERTS = 8
ALL = ("dp", "expert")


def nonlinear(gate, up, dhid):
    sig = jax.nn.sigmoid(gate)
    act = gate * sig
    hidden = (act * up).astype(jnp.bfloat16)
    d_up = (dhid * act).astype(jnp.bfloat16)
    d_gate = (dhid * up * sig * (1.0 + gate * (1.0 - sig))).astype(jnp.bfloat16)
    return (hidden, d_up, d_gate)


def contract_rows(left, right):
    return lax.dot_general(
        left, right, (((0,), (0,)), ((), ())), preferred_element_type=jnp.float32
    )


def _rows_body(dg_ref, du_ref, wg_ref, wu_ref, drows_ref):
    @pl.when(pl.program_id(0) == 0)
    def _():
        drows_ref[...] = jnp.zeros_like(drows_ref)
    nt = (((1,), (1,)), ((), ()))
    drows_ref[...] += lax.dot_general(
        wg_ref[...], dg_ref[...], nt, preferred_element_type=jnp.float32
    ) + lax.dot_general(wu_ref[...], du_ref[...], nt, preferred_element_type=jnp.float32)


def _grads_body(dg_ref, du_ref, h_ref, x_ref, y_ref, gg_ref, gu_ref, gd_ref):
    tn = (((0,), (0,)), ((), ()))
    x = x_ref[...]
    gg_ref[...] = lax.dot_general(x, dg_ref[...], tn, preferred_element_type=jnp.float32).astype(gg_ref.dtype)
    gu_ref[...] = lax.dot_general(x, du_ref[...], tn, preferred_element_type=jnp.float32).astype(gu_ref.dtype)
    gd_ref[...] = lax.dot_general(h_ref[...], y_ref[...], tn, preferred_element_type=jnp.float32).astype(gd_ref.dtype)


def backward_rows(gathered, w_gate, w_up):
    rows, ff = gathered.shape[1], gathered.shape[2]
    cols = w_gate.shape[0]
    tile = 1024 if ff % 1024 == 0 else ff

    def plane(p):
        return pl.BlockSpec((None, rows, tile), lambda k: (p, 0, k))

    return pl.pallas_call(
        _rows_body,
        grid=(ff // tile,),
        in_specs=[
            plane(2),
            plane(1),
            pl.BlockSpec((cols, tile), lambda k: (0, k)),
            pl.BlockSpec((cols, tile), lambda k: (0, k)),
        ],
        out_specs=pl.BlockSpec((cols, rows), lambda k: (0, 0)),
        out_shape=jax.ShapeDtypeStruct((cols, rows), jnp.float32),
        compiler_params=pltpu.CompilerParams(dimension_semantics=("arbitrary",)),
        cost_estimate=pl.CostEstimate(
            flops=4 * rows * ff * cols, transcendentals=0,
            bytes_accessed=2 * (2 * cols * ff + 2 * rows * ff) + 4 * rows * cols),
    )(gathered, gathered, w_gate, w_up)


def backward_grads(gathered, rows_in, rows_grad):
    rows, ff = gathered.shape[1], gathered.shape[2]
    cols = rows_in.shape[1]
    tile = 512 if ff % 512 == 0 else ff
    bf = jnp.bfloat16

    def plane(p):
        return pl.BlockSpec((None, rows, tile), lambda k: (p, 0, k))

    return pl.pallas_call(
        _grads_body,
        grid=(ff // tile,),
        in_specs=[
            plane(2),
            plane(1),
            plane(0),
            pl.BlockSpec((rows, cols), lambda k: (0, 0)),
            pl.BlockSpec((rows, cols), lambda k: (0, 0)),
        ],
        out_specs=[
            pl.BlockSpec((cols, tile), lambda k: (0, k)),
            pl.BlockSpec((cols, tile), lambda k: (0, k)),
            pl.BlockSpec((tile, cols), lambda k: (k, 0)),
        ],
        out_shape=[
            jax.ShapeDtypeStruct((cols, ff), bf),
            jax.ShapeDtypeStruct((cols, ff), bf),
            jax.ShapeDtypeStruct((ff, cols), bf),
        ],
        compiler_params=pltpu.CompilerParams(dimension_semantics=("parallel",)),
        cost_estimate=pl.CostEstimate(
            flops=6 * rows * ff * cols, transcendentals=0,
            bytes_accessed=2 * (3 * cols * ff + 3 * rows * ff + 2 * rows * cols)),
    )(gathered, gathered, gathered, rows_in, rows_grad)


def on_device(inputs, grad_out, labels, w_gate, w_up, w_down):
    members = lax.axis_size("expert")
    replicas = lax.axis_size("dp")
    group = members // EXPERTS
    tok_count = inputs.shape[0]
    width = inputs.shape[1]
    columns = width // replicas
    capacity = 3 * tok_count // (2 * EXPERTS)
    label_col = labels[:, 0]
    onehot = (label_col[:, None] == jnp.arange(EXPERTS, dtype=jnp.int32)[None, :]).astype(jnp.int32)
    before = jnp.cumsum(onehot, axis=0) - onehot
    rank_in = jnp.sum(before * onehot, axis=1)
    slot_ids = label_col * capacity + rank_in

    both = jnp.stack([inputs, grad_out])
    slots = jnp.zeros((2, EXPERTS * capacity, width), jnp.bfloat16).at[:, slot_ids].set(both)
    send = jnp.broadcast_to(
        jnp.transpose(slots.reshape(2, EXPERTS, capacity * width), (1, 0, 2))[:, None],
        (EXPERTS, group, 2, capacity * width),
    ).reshape(members, 2 * capacity * width)
    recv = lax.all_to_all(send, "expert", 0, 0, tiled=True)
    recv = recv.reshape(members * 2 * capacity, replicas, columns)
    recv = jnp.transpose(recv, (1, 0, 2)).reshape(replicas, members * 2 * capacity * columns)
    recv = lax.all_to_all(recv, "dp", 0, 0, tiled=True)
    recv = recv.reshape(replicas * members, 2, capacity, columns)
    rows_in = recv[:, 0].reshape(-1, columns)
    rows_grad = recv[:, 1].reshape(-1, columns)

    gate_part = jnp.dot(rows_in, w_gate, preferred_element_type=jnp.float32)
    up_part = jnp.dot(rows_in, w_up, preferred_element_type=jnp.float32)
    dhid_part = lax.dot_general(
        rows_grad, w_down, (((1,), (1,)), ((), ())), preferred_element_type=jnp.float32
    )
    parts = jnp.stack([gate_part, up_part, dhid_part]).astype(jnp.bfloat16)
    reduced = lax.psum_scatter(parts, "dp", scatter_dimension=2, tiled=True).astype(jnp.float32)
    hidden, d_up, d_gate = nonlinear(reduced[0], reduced[1], reduced[2])
    gathered = lax.all_gather(jnp.stack([hidden, d_up, d_gate]), "dp", axis=2, tiled=True)

    d_rows = backward_rows(gathered, w_gate, w_up).T
    back = d_rows.astype(jnp.bfloat16).reshape(replicas * members, capacity * columns)
    back = lax.all_to_all(back, ALL, 0, 0, tiled=True)
    back = back.reshape(replicas, EXPERTS, group, capacity, columns).astype(jnp.float32)
    summed = jnp.sum(back, axis=2)
    summed = jnp.transpose(summed, (1, 2, 0, 3)).reshape(EXPERTS * capacity, width)
    grad_in = summed[slot_ids].astype(jnp.bfloat16)
    grad_gate, grad_up, grad_down = backward_grads(gathered, rows_in, rows_grad)
    return (grad_in, grad_gate, grad_up, grad_down)


def solution(mesh):
    return jax.shard_map(
        on_device,
        mesh=mesh,
        in_specs=(
            P(ALL, None),
            P(ALL, None),
            P(ALL, None),
            P("dp", "expert"),
            P("dp", "expert"),
            P("expert", "dp"),
        ),
        out_specs=(
            P(ALL, None),
            P("dp", "expert"),
            P("dp", "expert"),
            P("expert", "dp"),
        ),
        check_vma=False,
    )
```

```python
import jax
import jax.numpy as jnp
from jax import lax
from jax.sharding import PartitionSpec as P
from jax.experimental import pallas as pl
from jax.experimental.pallas import tpu as pltpu

EXPERTS = 8
ALL = ("dp", "expert")


def nonlinear(gate, up, dhid):
    sig = jax.nn.sigmoid(gate)
    act = gate * sig
    hidden = (act * up).astype(jnp.bfloat16)
    d_up = (dhid * act).astype(jnp.bfloat16)
    d_gate = (dhid * up * sig * (1.0 + gate * (1.0 - sig))).astype(jnp.bfloat16)
    return (hidden, d_up, d_gate)


def contract_rows(left, right):
    return lax.dot_general(
        left, right, (((0,), (0,)), ((), ())), preferred_element_type=jnp.float32
    )


def _rows_body(dg_ref, du_ref, wg_ref, wu_ref, drows_ref):
    @pl.when(pl.program_id(0) == 0)
    def _():
        drows_ref[...] = jnp.zeros_like(drows_ref)
    nt = (((1,), (1,)), ((), ()))
    drows_ref[...] += lax.dot_general(
        wg_ref[...], dg_ref[...], nt, preferred_element_type=jnp.float32
    ) + lax.dot_general(wu_ref[...], du_ref[...], nt, preferred_element_type=jnp.float32)


def _grads_body(dg_ref, du_ref, h_ref, x_ref, y_ref, gg_ref, gu_ref, gd_ref):
    tn = (((0,), (0,)), ((), ()))
    x = x_ref[...]
    gg_ref[...] = lax.dot_general(x, dg_ref[...], tn, preferred_element_type=jnp.float32).astype(gg_ref.dtype)
    gu_ref[...] = lax.dot_general(x, du_ref[...], tn, preferred_element_type=jnp.float32).astype(gu_ref.dtype)
    gd_ref[...] = lax.dot_general(h_ref[...], y_ref[...], tn, preferred_element_type=jnp.float32).astype(gd_ref.dtype)


def backward_rows(gathered, w_gate, w_up):
    rows, ff = gathered.shape[1], gathered.shape[2]
    cols = w_gate.shape[0]
    tile = 1024 if ff % 1024 == 0 else ff

    def plane(p):
        return pl.BlockSpec((None, rows, tile), lambda k: (p, 0, k))

    return pl.pallas_call(
        _rows_body,
        grid=(ff // tile,),
        in_specs=[
            plane(2),
            plane(1),
            pl.BlockSpec((cols, tile), lambda k: (0, k)),
            pl.BlockSpec((cols, tile), lambda k: (0, k)),
        ],
        out_specs=pl.BlockSpec((cols, rows), lambda k: (0, 0)),
        out_shape=jax.ShapeDtypeStruct((cols, rows), jnp.float32),
        compiler_params=pltpu.CompilerParams(dimension_semantics=("arbitrary",)),
        cost_estimate=pl.CostEstimate(
            flops=4 * rows * ff * cols, transcendentals=0,
            bytes_accessed=2 * (2 * cols * ff + 2 * rows * ff) + 4 * rows * cols),
    )(gathered, gathered, w_gate, w_up)


def backward_grads(gathered, rows_in, rows_grad):
    rows, ff = gathered.shape[1], gathered.shape[2]
    cols = rows_in.shape[1]
    tile = 1024 if ff % 1024 == 0 else ff
    bf = jnp.bfloat16

    def plane(p):
        return pl.BlockSpec((None, rows, tile), lambda k: (p, 0, k))

    return pl.pallas_call(
        _grads_body,
        grid=(ff // tile,),
        in_specs=[
            plane(2),
            plane(1),
            plane(0),
            pl.BlockSpec((rows, cols), lambda k: (0, 0)),
            pl.BlockSpec((rows, cols), lambda k: (0, 0)),
        ],
        out_specs=[
            pl.BlockSpec((cols, tile), lambda k: (0, k)),
            pl.BlockSpec((cols, tile), lambda k: (0, k)),
            pl.BlockSpec((tile, cols), lambda k: (k, 0)),
        ],
        out_shape=[
            jax.ShapeDtypeStruct((cols, ff), bf),
            jax.ShapeDtypeStruct((cols, ff), bf),
            jax.ShapeDtypeStruct((ff, cols), bf),
        ],
        compiler_params=pltpu.CompilerParams(dimension_semantics=("parallel",)),
        cost_estimate=pl.CostEstimate(
            flops=6 * rows * ff * cols, transcendentals=0,
            bytes_accessed=2 * (3 * cols * ff + 3 * rows * ff + 2 * rows * cols)),
    )(gathered, gathered, gathered, rows_in, rows_grad)


def on_device(inputs, grad_out, labels, w_gate, w_up, w_down):
    members = lax.axis_size("expert")
    replicas = lax.axis_size("dp")
    group = members // EXPERTS
    tok_count = inputs.shape[0]
    width = inputs.shape[1]
    columns = width // replicas
    capacity = 3 * tok_count // (2 * EXPERTS)
    label_col = labels[:, 0]
    onehot = (label_col[:, None] == jnp.arange(EXPERTS, dtype=jnp.int32)[None, :]).astype(jnp.int32)
    before = jnp.cumsum(onehot, axis=0) - onehot
    rank_in = jnp.sum(before * onehot, axis=1)
    slot_ids = label_col * capacity + rank_in

    both = jnp.stack([inputs, grad_out])
    slots = jnp.zeros((2, EXPERTS * capacity, width), jnp.bfloat16).at[:, slot_ids].set(both)
    send = slots.reshape(2, EXPERTS, capacity, replicas, columns)
    send = jnp.transpose(send, (3, 1, 0, 2, 4))
    send = jnp.broadcast_to(
        send[:, :, None], (replicas, EXPERTS, group, 2, capacity, columns)
    ).reshape(replicas * members, 2 * capacity * columns)
    recv = lax.all_to_all(send, ALL, 0, 0, tiled=True)
    recv = recv.reshape(replicas * members, 2, capacity, columns)
    rows_in = recv[:, 0].reshape(-1, columns)
    rows_grad = recv[:, 1].reshape(-1, columns)

    gate_part = jnp.dot(rows_in, w_gate, preferred_element_type=jnp.float32)
    up_part = jnp.dot(rows_in, w_up, preferred_element_type=jnp.float32)
    dhid_part = lax.dot_general(
        rows_grad, w_down, (((1,), (1,)), ((), ())), preferred_element_type=jnp.float32
    )
    parts = jnp.stack([gate_part, up_part, dhid_part]).astype(jnp.bfloat16)
    reduced = lax.psum_scatter(parts, "dp", scatter_dimension=2, tiled=True).astype(jnp.float32)
    hidden, d_up, d_gate = nonlinear(reduced[0], reduced[1], reduced[2])
    gathered = lax.all_gather(jnp.stack([hidden, d_up, d_gate]), "dp", axis=2, tiled=True)

    d_rows = backward_rows(gathered, w_gate, w_up).T
    back = d_rows.astype(jnp.bfloat16).reshape(replicas * members, capacity * columns)
    back = lax.all_to_all(back, ALL, 0, 0, tiled=True)
    back = back.reshape(replicas, EXPERTS, group, capacity, columns).astype(jnp.float32)
    summed = jnp.sum(back, axis=2)
    summed = jnp.transpose(summed, (1, 2, 0, 3)).reshape(EXPERTS * capacity, width)
    grad_in = summed[slot_ids].astype(jnp.bfloat16)
    grad_gate, grad_up, grad_down = backward_grads(gathered, rows_in, rows_grad)
    return (grad_in, grad_gate, grad_up, grad_down)


def solution(mesh):
    return jax.shard_map(
        on_device,
        mesh=mesh,
        in_specs=(
            P(ALL, None),
            P(ALL, None),
            P(ALL, None),
            P("dp", "expert"),
            P("dp", "expert"),
            P("expert", "dp"),
        ),
        out_specs=(
            P(ALL, None),
            P("dp", "expert"),
            P("dp", "expert"),
            P("expert", "dp"),
        ),
        check_vma=False,
    )
```

```python
import jax
import jax.numpy as jnp
from jax import lax
from jax.sharding import PartitionSpec as P
from jax.experimental import pallas as pl
from jax.experimental.pallas import tpu as pltpu

EXPERTS = 8
ALL = ("dp", "expert")


def nonlinear(gate, up, dhid):
    sig = jax.nn.sigmoid(gate)
    act = gate * sig
    hidden = (act * up).astype(jnp.bfloat16)
    d_up = (dhid * act).astype(jnp.bfloat16)
    d_gate = (dhid * up * sig * (1.0 + gate * (1.0 - sig))).astype(jnp.bfloat16)
    return (hidden, d_up, d_gate)


def contract_rows(left, right):
    return lax.dot_general(
        left, right, (((0,), (0,)), ((), ())), preferred_element_type=jnp.float32
    )


def _fwd_body(x_ref, y_ref, wg_ref, wu_ref, wd_ref, out_ref):
    x = x_ref[...]
    nt = (((1,), (1,)), ((), ()))
    out_ref[0] = jnp.dot(x, wg_ref[...], preferred_element_type=jnp.float32).astype(out_ref.dtype)
    out_ref[1] = jnp.dot(x, wu_ref[...], preferred_element_type=jnp.float32).astype(out_ref.dtype)
    out_ref[2] = lax.dot_general(
        y_ref[...], wd_ref[...], nt, preferred_element_type=jnp.float32
    ).astype(out_ref.dtype)


def forward_parts(rows_in, rows_grad, w_gate, w_up, w_down):
    rows, cols = rows_in.shape
    ff = w_gate.shape[1]
    tile = 1024 if ff % 1024 == 0 else ff
    return pl.pallas_call(
        _fwd_body,
        grid=(ff // tile,),
        in_specs=[
            pl.BlockSpec((rows, cols), lambda k: (0, 0)),
            pl.BlockSpec((rows, cols), lambda k: (0, 0)),
            pl.BlockSpec((cols, tile), lambda k: (0, k)),
            pl.BlockSpec((cols, tile), lambda k: (0, k)),
            pl.BlockSpec((tile, cols), lambda k: (k, 0)),
        ],
        out_specs=pl.BlockSpec((3, rows, tile), lambda k: (0, 0, k)),
        out_shape=jax.ShapeDtypeStruct((3, rows, ff), jnp.bfloat16),
        compiler_params=pltpu.CompilerParams(dimension_semantics=("parallel",)),
        cost_estimate=pl.CostEstimate(
            flops=6 * rows * ff * cols, transcendentals=0,
            bytes_accessed=2 * (3 * cols * ff + 3 * rows * ff + 2 * rows * cols)),
    )(rows_in, rows_grad, w_gate, w_up, w_down)


def _rows_body(dg_ref, du_ref, wg_ref, wu_ref, drows_ref):
    @pl.when(pl.program_id(0) == 0)
    def _():
        drows_ref[...] = jnp.zeros_like(drows_ref)
    nt = (((1,), (1,)), ((), ()))
    drows_ref[...] += lax.dot_general(
        wg_ref[...], dg_ref[...], nt, preferred_element_type=jnp.float32
    ) + lax.dot_general(wu_ref[...], du_ref[...], nt, preferred_element_type=jnp.float32)


def _grads_body(dg_ref, du_ref, h_ref, x_ref, y_ref, gg_ref, gu_ref, gd_ref):
    tn = (((0,), (0,)), ((), ()))
    x = x_ref[...]
    gg_ref[...] = lax.dot_general(x, dg_ref[...], tn, preferred_element_type=jnp.float32).astype(gg_ref.dtype)
    gu_ref[...] = lax.dot_general(x, du_ref[...], tn, preferred_element_type=jnp.float32).astype(gu_ref.dtype)
    gd_ref[...] = lax.dot_general(h_ref[...], y_ref[...], tn, preferred_element_type=jnp.float32).astype(gd_ref.dtype)


def backward_rows(gathered, w_gate, w_up):
    rows, ff = gathered.shape[1], gathered.shape[2]
    cols = w_gate.shape[0]
    tile = 1024 if ff % 1024 == 0 else ff

    def plane(p):
        return pl.BlockSpec((None, rows, tile), lambda k: (p, 0, k))

    return pl.pallas_call(
        _rows_body,
        grid=(ff // tile,),
        in_specs=[
            plane(2),
            plane(1),
            pl.BlockSpec((cols, tile), lambda k: (0, k)),
            pl.BlockSpec((cols, tile), lambda k: (0, k)),
        ],
        out_specs=pl.BlockSpec((cols, rows), lambda k: (0, 0)),
        out_shape=jax.ShapeDtypeStruct((cols, rows), jnp.float32),
        compiler_params=pltpu.CompilerParams(dimension_semantics=("arbitrary",)),
        cost_estimate=pl.CostEstimate(
            flops=4 * rows * ff * cols, transcendentals=0,
            bytes_accessed=2 * (2 * cols * ff + 2 * rows * ff) + 4 * rows * cols),
    )(gathered, gathered, w_gate, w_up)


def backward_grads(gathered, rows_in, rows_grad):
    rows, ff = gathered.shape[1], gathered.shape[2]
    cols = rows_in.shape[1]
    tile = 1024 if ff % 1024 == 0 else ff
    bf = jnp.bfloat16

    def plane(p):
        return pl.BlockSpec((None, rows, tile), lambda k: (p, 0, k))

    return pl.pallas_call(
        _grads_body,
        grid=(ff // tile,),
        in_specs=[
            plane(2),
            plane(1),
            plane(0),
            pl.BlockSpec((rows, cols), lambda k: (0, 0)),
            pl.BlockSpec((rows, cols), lambda k: (0, 0)),
        ],
        out_specs=[
            pl.BlockSpec((cols, tile), lambda k: (0, k)),
            pl.BlockSpec((cols, tile), lambda k: (0, k)),
            pl.BlockSpec((tile, cols), lambda k: (k, 0)),
        ],
        out_shape=[
            jax.ShapeDtypeStruct((cols, ff), bf),
            jax.ShapeDtypeStruct((cols, ff), bf),
            jax.ShapeDtypeStruct((ff, cols), bf),
        ],
        compiler_params=pltpu.CompilerParams(dimension_semantics=("parallel",)),
        cost_estimate=pl.CostEstimate(
            flops=6 * rows * ff * cols, transcendentals=0,
            bytes_accessed=2 * (3 * cols * ff + 3 * rows * ff + 2 * rows * cols)),
    )(gathered, gathered, gathered, rows_in, rows_grad)


def on_device(inputs, grad_out, labels, w_gate, w_up, w_down):
    members = lax.axis_size("expert")
    replicas = lax.axis_size("dp")
    group = members // EXPERTS
    tok_count = inputs.shape[0]
    width = inputs.shape[1]
    columns = width // replicas
    capacity = 3 * tok_count // (2 * EXPERTS)
    label_col = labels[:, 0]
    onehot = (label_col[:, None] == jnp.arange(EXPERTS, dtype=jnp.int32)[None, :]).astype(jnp.int32)
    before = jnp.cumsum(onehot, axis=0) - onehot
    rank_in = jnp.sum(before * onehot, axis=1)
    slot_ids = label_col * capacity + rank_in

    both = jnp.stack([inputs, grad_out])
    slots = jnp.zeros((2, EXPERTS * capacity, width), jnp.bfloat16).at[:, slot_ids].set(both)
    send = slots.reshape(2, EXPERTS, capacity, replicas, columns)
    send = jnp.transpose(send, (3, 1, 0, 2, 4))
    send = jnp.broadcast_to(
        send[:, :, None], (replicas, EXPERTS, group, 2, capacity, columns)
    ).reshape(replicas * members, 2 * capacity * columns)
    recv = lax.all_to_all(send, ALL, 0, 0, tiled=True)
    recv = recv.reshape(replicas * members, 2, capacity, columns)
    rows_in = recv[:, 0].reshape(-1, columns)
    rows_grad = recv[:, 1].reshape(-1, columns)

    parts = forward_parts(rows_in, rows_grad, w_gate, w_up, w_down)
    reduced = lax.psum_scatter(parts, "dp", scatter_dimension=2, tiled=True).astype(jnp.float32)
    hidden, d_up, d_gate = nonlinear(reduced[0], reduced[1], reduced[2])
    gathered = lax.all_gather(jnp.stack([hidden, d_up, d_gate]), "dp", axis=2, tiled=True)

    d_rows = backward_rows(gathered, w_gate, w_up).T
    back = d_rows.astype(jnp.bfloat16).reshape(replicas * members, capacity * columns)
    back = lax.all_to_all(back, ALL, 0, 0, tiled=True)
    back = back.reshape(replicas, EXPERTS, group, capacity, columns).astype(jnp.float32)
    summed = jnp.sum(back, axis=2)
    summed = jnp.transpose(summed, (1, 2, 0, 3)).reshape(EXPERTS * capacity, width)
    grad_in = summed[slot_ids].astype(jnp.bfloat16)
    grad_gate, grad_up, grad_down = backward_grads(gathered, rows_in, rows_grad)
    return (grad_in, grad_gate, grad_up, grad_down)


def solution(mesh):
    return jax.shard_map(
        on_device,
        mesh=mesh,
        in_specs=(
            P(ALL, None),
            P(ALL, None),
            P(ALL, None),
            P("dp", "expert"),
            P("dp", "expert"),
            P("expert", "dp"),
        ),
        out_specs=(
            P(ALL, None),
            P("dp", "expert"),
            P("dp", "expert"),
            P("expert", "dp"),
        ),
        check_vma=False,
    )
```

```python
import jax
import jax.numpy as jnp
from jax import lax
from jax.sharding import PartitionSpec as P
from jax.experimental import pallas as pl
from jax.experimental.pallas import tpu as pltpu

EXPERTS = 8
ALL = ("dp", "expert")


def nonlinear(gate, up, dhid):
    sig = jax.nn.sigmoid(gate)
    act = gate * sig
    hidden = (act * up).astype(jnp.bfloat16)
    d_up = (dhid * act).astype(jnp.bfloat16)
    d_gate = (dhid * up * sig * (1.0 + gate * (1.0 - sig))).astype(jnp.bfloat16)
    return (hidden, d_up, d_gate)


def contract_rows(left, right):
    return lax.dot_general(
        left, right, (((0,), (0,)), ((), ())), preferred_element_type=jnp.float32
    )


def _fwd_body(x_ref, y_ref, wg_ref, wu_ref, wd_ref, out_ref):
    x = x_ref[...]
    nt = (((1,), (1,)), ((), ()))
    out_ref[0] = jnp.dot(x, wg_ref[...], preferred_element_type=jnp.float32).astype(out_ref.dtype)
    out_ref[1] = jnp.dot(x, wu_ref[...], preferred_element_type=jnp.float32).astype(out_ref.dtype)
    out_ref[2] = lax.dot_general(
        y_ref[...], wd_ref[...], nt, preferred_element_type=jnp.float32
    ).astype(out_ref.dtype)


def forward_parts(rows_in, rows_grad, w_gate, w_up, w_down):
    rows, cols = rows_in.shape
    ff = w_gate.shape[1]
    tile = 1024 if ff % 1024 == 0 else ff
    return pl.pallas_call(
        _fwd_body,
        grid=(ff // tile,),
        in_specs=[
            pl.BlockSpec((rows, cols), lambda k: (0, 0)),
            pl.BlockSpec((rows, cols), lambda k: (0, 0)),
            pl.BlockSpec((cols, tile), lambda k: (0, k)),
            pl.BlockSpec((cols, tile), lambda k: (0, k)),
            pl.BlockSpec((tile, cols), lambda k: (k, 0)),
        ],
        out_specs=pl.BlockSpec((3, rows, tile), lambda k: (0, 0, k)),
        out_shape=jax.ShapeDtypeStruct((3, rows, ff), jnp.bfloat16),
        compiler_params=pltpu.CompilerParams(dimension_semantics=("parallel",)),
        cost_estimate=pl.CostEstimate(
            flops=6 * rows * ff * cols, transcendentals=0,
            bytes_accessed=2 * (3 * cols * ff + 3 * rows * ff + 2 * rows * cols)),
    )(rows_in, rows_grad, w_gate, w_up, w_down)


def _rows_body(dg_ref, du_ref, wg_ref, wu_ref, drows_ref):
    @pl.when(pl.program_id(0) == 0)
    def _():
        drows_ref[...] = jnp.zeros_like(drows_ref)
    nt = (((1,), (1,)), ((), ()))
    drows_ref[...] += lax.dot_general(
        wg_ref[...], dg_ref[...], nt, preferred_element_type=jnp.float32
    ) + lax.dot_general(wu_ref[...], du_ref[...], nt, preferred_element_type=jnp.float32)


def _grads_body(dg_ref, du_ref, h_ref, x_ref, y_ref, gg_ref, gu_ref, gd_ref):
    tn = (((0,), (0,)), ((), ()))
    x = x_ref[...]
    gg_ref[...] = lax.dot_general(x, dg_ref[...], tn, preferred_element_type=jnp.float32).astype(gg_ref.dtype)
    gu_ref[...] = lax.dot_general(x, du_ref[...], tn, preferred_element_type=jnp.float32).astype(gu_ref.dtype)
    gd_ref[...] = lax.dot_general(h_ref[...], y_ref[...], tn, preferred_element_type=jnp.float32).astype(gd_ref.dtype)


def backward_rows(pair, w_gate, w_up):
    rows, ff = pair.shape[1], pair.shape[2]
    cols = w_gate.shape[0]
    tile = 1024 if ff % 1024 == 0 else ff

    def plane(p):
        return pl.BlockSpec((None, rows, tile), lambda k: (p, 0, k))

    return pl.pallas_call(
        _rows_body,
        grid=(ff // tile,),
        in_specs=[
            plane(1),
            plane(0),
            pl.BlockSpec((cols, tile), lambda k: (0, k)),
            pl.BlockSpec((cols, tile), lambda k: (0, k)),
        ],
        out_specs=pl.BlockSpec((cols, rows), lambda k: (0, 0)),
        out_shape=jax.ShapeDtypeStruct((cols, rows), jnp.float32),
        compiler_params=pltpu.CompilerParams(dimension_semantics=("arbitrary",)),
        cost_estimate=pl.CostEstimate(
            flops=4 * rows * ff * cols, transcendentals=0,
            bytes_accessed=2 * (2 * cols * ff + 2 * rows * ff) + 4 * rows * cols),
    )(pair, pair, w_gate, w_up)


def backward_grads(pair, hidden, rows_in, rows_grad):
    rows, ff = pair.shape[1], pair.shape[2]
    cols = rows_in.shape[1]
    tile = 1024 if ff % 1024 == 0 else ff
    bf = jnp.bfloat16

    def plane(p):
        return pl.BlockSpec((None, rows, tile), lambda k: (p, 0, k))

    return pl.pallas_call(
        _grads_body,
        grid=(ff // tile,),
        in_specs=[
            plane(1),
            plane(0),
            pl.BlockSpec((None, rows, tile), lambda k: (0, 0, k)),
            pl.BlockSpec((rows, cols), lambda k: (0, 0)),
            pl.BlockSpec((rows, cols), lambda k: (0, 0)),
        ],
        out_specs=[
            pl.BlockSpec((cols, tile), lambda k: (0, k)),
            pl.BlockSpec((cols, tile), lambda k: (0, k)),
            pl.BlockSpec((tile, cols), lambda k: (k, 0)),
        ],
        out_shape=[
            jax.ShapeDtypeStruct((cols, ff), bf),
            jax.ShapeDtypeStruct((cols, ff), bf),
            jax.ShapeDtypeStruct((ff, cols), bf),
        ],
        compiler_params=pltpu.CompilerParams(dimension_semantics=("parallel",)),
        cost_estimate=pl.CostEstimate(
            flops=6 * rows * ff * cols, transcendentals=0,
            bytes_accessed=2 * (3 * cols * ff + 3 * rows * ff + 2 * rows * cols)),
    )(pair, pair, hidden, rows_in, rows_grad)


def on_device(inputs, grad_out, labels, w_gate, w_up, w_down):
    members = lax.axis_size("expert")
    replicas = lax.axis_size("dp")
    group = members // EXPERTS
    tok_count = inputs.shape[0]
    width = inputs.shape[1]
    columns = width // replicas
    capacity = 3 * tok_count // (2 * EXPERTS)
    label_col = labels[:, 0]
    onehot = (label_col[:, None] == jnp.arange(EXPERTS, dtype=jnp.int32)[None, :]).astype(jnp.int32)
    before = jnp.cumsum(onehot, axis=0) - onehot
    rank_in = jnp.sum(before * onehot, axis=1)
    slot_ids = label_col * capacity + rank_in

    both = jnp.stack([inputs, grad_out])
    slots = jnp.zeros((2, EXPERTS * capacity, width), jnp.bfloat16).at[:, slot_ids].set(both)
    send = slots.reshape(2, EXPERTS, capacity, replicas, columns)
    send = jnp.transpose(send, (3, 1, 0, 2, 4))
    send = jnp.broadcast_to(
        send[:, :, None], (replicas, EXPERTS, group, 2, capacity, columns)
    ).reshape(replicas * members, 2 * capacity * columns)
    recv = lax.all_to_all(send, ALL, 0, 0, tiled=True)
    recv = recv.reshape(replicas * members, 2, capacity, columns)
    rows_in = recv[:, 0].reshape(-1, columns)
    rows_grad = recv[:, 1].reshape(-1, columns)

    parts = forward_parts(rows_in, rows_grad, w_gate, w_up, w_down)
    reduced = lax.psum_scatter(parts, "dp", scatter_dimension=2, tiled=True).astype(jnp.float32)
    hidden, d_up, d_gate = nonlinear(reduced[0], reduced[1], reduced[2])
    pair = lax.all_gather(jnp.stack([d_up, d_gate]), "dp", axis=2, tiled=True)
    hidden = lax.all_gather(hidden[None], "dp", axis=2, tiled=True)

    d_rows = backward_rows(pair, w_gate, w_up).T
    back = d_rows.astype(jnp.bfloat16).reshape(replicas * members, capacity * columns)
    back = lax.all_to_all(back, ALL, 0, 0, tiled=True)
    back = back.reshape(replicas, EXPERTS, group, capacity, columns).astype(jnp.float32)
    summed = jnp.sum(back, axis=2)
    summed = jnp.transpose(summed, (1, 2, 0, 3)).reshape(EXPERTS * capacity, width)
    grad_in = summed[slot_ids].astype(jnp.bfloat16)
    grad_gate, grad_up, grad_down = backward_grads(pair, hidden, rows_in, rows_grad)
    return (grad_in, grad_gate, grad_up, grad_down)


def solution(mesh):
    return jax.shard_map(
        on_device,
        mesh=mesh,
        in_specs=(
            P(ALL, None),
            P(ALL, None),
            P(ALL, None),
            P("dp", "expert"),
            P("dp", "expert"),
            P("expert", "dp"),
        ),
        out_specs=(
            P(ALL, None),
            P("dp", "expert"),
            P("dp", "expert"),
            P("expert", "dp"),
        ),
        check_vma=False,
    )
```

```python
import jax
import jax.numpy as jnp
from jax import lax
from jax.sharding import PartitionSpec as P
from jax.experimental import pallas as pl
from jax.experimental.pallas import tpu as pltpu

EXPERTS = 8
ALL = ("dp", "expert")


def nonlinear(gate, up, dhid):
    sig = jax.nn.sigmoid(gate)
    act = gate * sig
    hidden = (act * up).astype(jnp.bfloat16)
    d_up = (dhid * act).astype(jnp.bfloat16)
    d_gate = (dhid * up * sig * (1.0 + gate * (1.0 - sig))).astype(jnp.bfloat16)
    return (hidden, d_up, d_gate)


def contract_rows(left, right):
    return lax.dot_general(
        left, right, (((0,), (0,)), ((), ())), preferred_element_type=jnp.float32
    )


def _fwd_body(x_ref, y_ref, wg_ref, wu_ref, wd_ref, out_ref):
    x = x_ref[...]
    nt = (((1,), (1,)), ((), ()))
    out_ref[0] = jnp.dot(x, wg_ref[...], preferred_element_type=jnp.float32).astype(out_ref.dtype)
    out_ref[1] = jnp.dot(x, wu_ref[...], preferred_element_type=jnp.float32).astype(out_ref.dtype)
    out_ref[2] = lax.dot_general(
        y_ref[...], wd_ref[...], nt, preferred_element_type=jnp.float32
    ).astype(out_ref.dtype)


def forward_parts(rows_in, rows_grad, w_gate, w_up, w_down):
    rows, cols = rows_in.shape
    ff = w_gate.shape[1]
    tile = 1024 if ff % 1024 == 0 else ff
    return pl.pallas_call(
        _fwd_body,
        grid=(ff // tile,),
        in_specs=[
            pl.BlockSpec((rows, cols), lambda k: (0, 0)),
            pl.BlockSpec((rows, cols), lambda k: (0, 0)),
            pl.BlockSpec((cols, tile), lambda k: (0, k)),
            pl.BlockSpec((cols, tile), lambda k: (0, k)),
            pl.BlockSpec((tile, cols), lambda k: (k, 0)),
        ],
        out_specs=pl.BlockSpec((3, rows, tile), lambda k: (0, 0, k)),
        out_shape=jax.ShapeDtypeStruct((3, rows, ff), jnp.bfloat16),
        compiler_params=pltpu.CompilerParams(dimension_semantics=("parallel",)),
        cost_estimate=pl.CostEstimate(
            flops=6 * rows * ff * cols, transcendentals=0,
            bytes_accessed=2 * (3 * cols * ff + 3 * rows * ff + 2 * rows * cols)),
    )(rows_in, rows_grad, w_gate, w_up, w_down)


def _rows_body(dg_ref, du_ref, wg_ref, wu_ref, out_ref, acc_ref):
    @pl.when(pl.program_id(0) == 0)
    def _():
        acc_ref[...] = jnp.zeros_like(acc_ref)
    nt = (((1,), (1,)), ((), ()))
    acc_ref[...] += lax.dot_general(
        dg_ref[...], wg_ref[...], nt, preferred_element_type=jnp.float32
    ) + lax.dot_general(du_ref[...], wu_ref[...], nt, preferred_element_type=jnp.float32)

    @pl.when(pl.program_id(0) == pl.num_programs(0) - 1)
    def _():
        out_ref[...] = acc_ref[...].astype(out_ref.dtype)


def _grads_body(dg_ref, du_ref, h_ref, x_ref, y_ref, gg_ref, gu_ref, gd_ref):
    tn = (((0,), (0,)), ((), ()))
    x = x_ref[...]
    gg_ref[...] = lax.dot_general(x, dg_ref[...], tn, preferred_element_type=jnp.float32).astype(gg_ref.dtype)
    gu_ref[...] = lax.dot_general(x, du_ref[...], tn, preferred_element_type=jnp.float32).astype(gu_ref.dtype)
    gd_ref[...] = lax.dot_general(h_ref[...], y_ref[...], tn, preferred_element_type=jnp.float32).astype(gd_ref.dtype)


def backward_rows(pair, w_gate, w_up):
    rows, ff = pair.shape[1], pair.shape[2]
    cols = w_gate.shape[0]
    tile = 1024 if ff % 1024 == 0 else ff

    def plane(p):
        return pl.BlockSpec((None, rows, tile), lambda k: (p, 0, k))

    return pl.pallas_call(
        _rows_body,
        grid=(ff // tile,),
        in_specs=[
            plane(1),
            plane(0),
            pl.BlockSpec((cols, tile), lambda k: (0, k)),
            pl.BlockSpec((cols, tile), lambda k: (0, k)),
        ],
        out_specs=pl.BlockSpec((rows, cols), lambda k: (0, 0)),
        out_shape=jax.ShapeDtypeStruct((rows, cols), jnp.bfloat16),
        scratch_shapes=[pltpu.VMEM((rows, cols), jnp.float32)],
        compiler_params=pltpu.CompilerParams(dimension_semantics=("arbitrary",)),
        cost_estimate=pl.CostEstimate(
            flops=4 * rows * ff * cols, transcendentals=0,
            bytes_accessed=2 * (2 * cols * ff + 2 * rows * ff) + 4 * rows * cols),
    )(pair, pair, w_gate, w_up)


def backward_grads(pair, hidden, rows_in, rows_grad):
    rows, ff = pair.shape[1], pair.shape[2]
    cols = rows_in.shape[1]
    tile = 1024 if ff % 1024 == 0 else ff
    bf = jnp.bfloat16

    def plane(p):
        return pl.BlockSpec((None, rows, tile), lambda k: (p, 0, k))

    return pl.pallas_call(
        _grads_body,
        grid=(ff // tile,),
        in_specs=[
            plane(1),
            plane(0),
            pl.BlockSpec((None, rows, tile), lambda k: (0, 0, k)),
            pl.BlockSpec((rows, cols), lambda k: (0, 0)),
            pl.BlockSpec((rows, cols), lambda k: (0, 0)),
        ],
        out_specs=[
            pl.BlockSpec((cols, tile), lambda k: (0, k)),
            pl.BlockSpec((cols, tile), lambda k: (0, k)),
            pl.BlockSpec((tile, cols), lambda k: (k, 0)),
        ],
        out_shape=[
            jax.ShapeDtypeStruct((cols, ff), bf),
            jax.ShapeDtypeStruct((cols, ff), bf),
            jax.ShapeDtypeStruct((ff, cols), bf),
        ],
        compiler_params=pltpu.CompilerParams(dimension_semantics=("parallel",)),
        cost_estimate=pl.CostEstimate(
            flops=6 * rows * ff * cols, transcendentals=0,
            bytes_accessed=2 * (3 * cols * ff + 3 * rows * ff + 2 * rows * cols)),
    )(pair, pair, hidden, rows_in, rows_grad)


def on_device(inputs, grad_out, labels, w_gate, w_up, w_down):
    members = lax.axis_size("expert")
    replicas = lax.axis_size("dp")
    group = members // EXPERTS
    tok_count = inputs.shape[0]
    width = inputs.shape[1]
    columns = width // replicas
    capacity = 3 * tok_count // (2 * EXPERTS)
    label_col = labels[:, 0]
    onehot = (label_col[:, None] == jnp.arange(EXPERTS, dtype=jnp.int32)[None, :]).astype(jnp.int32)
    before = jnp.cumsum(onehot, axis=0) - onehot
    rank_in = jnp.sum(before * onehot, axis=1)
    slot_ids = label_col * capacity + rank_in

    both = jnp.stack([inputs, grad_out])
    slots = jnp.zeros((2, EXPERTS * capacity, width), jnp.bfloat16).at[:, slot_ids].set(both)
    send = slots.reshape(2, EXPERTS, capacity, replicas, columns)
    send = jnp.transpose(send, (3, 1, 0, 2, 4))
    send = jnp.broadcast_to(
        send[:, :, None], (replicas, EXPERTS, group, 2, capacity, columns)
    ).reshape(replicas * members, 2 * capacity * columns)
    recv = lax.all_to_all(send, ALL, 0, 0, tiled=True)
    recv = recv.reshape(replicas * members, 2, capacity, columns)
    rows_in = recv[:, 0].reshape(-1, columns)
    rows_grad = recv[:, 1].reshape(-1, columns)

    parts = forward_parts(rows_in, rows_grad, w_gate, w_up, w_down)
    reduced = lax.psum_scatter(parts, "dp", scatter_dimension=2, tiled=True).astype(jnp.float32)
    hidden, d_up, d_gate = nonlinear(reduced[0], reduced[1], reduced[2])
    pair = lax.all_gather(jnp.stack([d_up, d_gate]), "dp", axis=2, tiled=True)
    hidden = lax.all_gather(hidden[None], "dp", axis=2, tiled=True)

    d_rows = backward_rows(pair, w_gate, w_up)
    back = d_rows.astype(jnp.bfloat16).reshape(replicas * members, capacity * columns)
    back = lax.all_to_all(back, ALL, 0, 0, tiled=True)
    back = back.reshape(replicas, EXPERTS, group, capacity, columns).astype(jnp.float32)
    summed = jnp.sum(back, axis=2)
    summed = jnp.transpose(summed, (1, 2, 0, 3)).reshape(EXPERTS * capacity, width)
    grad_in = summed[slot_ids].astype(jnp.bfloat16)
    grad_gate, grad_up, grad_down = backward_grads(pair, hidden, rows_in, rows_grad)
    return (grad_in, grad_gate, grad_up, grad_down)


def solution(mesh):
    return jax.shard_map(
        on_device,
        mesh=mesh,
        in_specs=(
            P(ALL, None),
            P(ALL, None),
            P(ALL, None),
            P("dp", "expert"),
            P("dp", "expert"),
            P("expert", "dp"),
        ),
        out_specs=(
            P(ALL, None),
            P("dp", "expert"),
            P("dp", "expert"),
            P("expert", "dp"),
        ),
        check_vma=False,
    )
```

```python
import jax
import jax.numpy as jnp
from jax import lax
from jax.sharding import PartitionSpec as P
from jax.experimental import pallas as pl
from jax.experimental.pallas import tpu as pltpu

EXPERTS = 8
ALL = ("dp", "expert")


def nonlinear(gate, up, dhid):
    sig = jax.nn.sigmoid(gate)
    act = gate * sig
    hidden = (act * up).astype(jnp.bfloat16)
    d_up = (dhid * act).astype(jnp.bfloat16)
    d_gate = (dhid * up * sig * (1.0 + gate * (1.0 - sig))).astype(jnp.bfloat16)
    return (hidden, d_up, d_gate)


def contract_rows(left, right):
    return lax.dot_general(
        left, right, (((0,), (0,)), ((), ())), preferred_element_type=jnp.float32
    )


def _nonlinear_body(r_ref, pair_ref, h_ref):
    gate = r_ref[0].astype(jnp.float32)
    up = r_ref[1].astype(jnp.float32)
    dhid = r_ref[2].astype(jnp.float32)
    sig = 1.0 / (1.0 + jnp.exp(-gate))
    act = gate * sig
    h_ref[0] = (act * up).astype(h_ref.dtype)
    pair_ref[0] = (dhid * act).astype(pair_ref.dtype)
    pair_ref[1] = (dhid * up * sig * (1.0 + gate * (1.0 - sig))).astype(pair_ref.dtype)


def nonlinear_stacks(reduced):
    _, rows, n = reduced.shape
    return pl.pallas_call(
        _nonlinear_body,
        out_shape=[
            jax.ShapeDtypeStruct((2, rows, n), jnp.bfloat16),
            jax.ShapeDtypeStruct((1, rows, n), jnp.bfloat16),
        ],
    )(reduced)


def _fwd_body(x_ref, y_ref, wg_ref, wu_ref, wd_ref, out_ref):
    x = x_ref[...]
    nt = (((1,), (1,)), ((), ()))
    out_ref[0] = jnp.dot(x, wg_ref[...], preferred_element_type=jnp.float32).astype(out_ref.dtype)
    out_ref[1] = jnp.dot(x, wu_ref[...], preferred_element_type=jnp.float32).astype(out_ref.dtype)
    out_ref[2] = lax.dot_general(
        y_ref[...], wd_ref[...], nt, preferred_element_type=jnp.float32
    ).astype(out_ref.dtype)


def forward_parts(rows_in, rows_grad, w_gate, w_up, w_down):
    rows, cols = rows_in.shape
    ff = w_gate.shape[1]
    tile = 1024 if ff % 1024 == 0 else ff
    return pl.pallas_call(
        _fwd_body,
        grid=(ff // tile,),
        in_specs=[
            pl.BlockSpec((rows, cols), lambda k: (0, 0)),
            pl.BlockSpec((rows, cols), lambda k: (0, 0)),
            pl.BlockSpec((cols, tile), lambda k: (0, k)),
            pl.BlockSpec((cols, tile), lambda k: (0, k)),
            pl.BlockSpec((tile, cols), lambda k: (k, 0)),
        ],
        out_specs=pl.BlockSpec((3, rows, tile), lambda k: (0, 0, k)),
        out_shape=jax.ShapeDtypeStruct((3, rows, ff), jnp.bfloat16),
        compiler_params=pltpu.CompilerParams(dimension_semantics=("parallel",)),
        cost_estimate=pl.CostEstimate(
            flops=6 * rows * ff * cols, transcendentals=0,
            bytes_accessed=2 * (3 * cols * ff + 3 * rows * ff + 2 * rows * cols)),
    )(rows_in, rows_grad, w_gate, w_up, w_down)


def _rows_body(dg_ref, du_ref, wg_ref, wu_ref, drows_ref):
    @pl.when(pl.program_id(0) == 0)
    def _():
        drows_ref[...] = jnp.zeros_like(drows_ref)
    nt = (((1,), (1,)), ((), ()))
    drows_ref[...] += lax.dot_general(
        wg_ref[...], dg_ref[...], nt, preferred_element_type=jnp.float32
    ) + lax.dot_general(wu_ref[...], du_ref[...], nt, preferred_element_type=jnp.float32)


def _grads_body(dg_ref, du_ref, h_ref, x_ref, y_ref, gg_ref, gu_ref, gd_ref):
    tn = (((0,), (0,)), ((), ()))
    x = x_ref[...]
    gg_ref[...] = lax.dot_general(x, dg_ref[...], tn, preferred_element_type=jnp.float32).astype(gg_ref.dtype)
    gu_ref[...] = lax.dot_general(x, du_ref[...], tn, preferred_element_type=jnp.float32).astype(gu_ref.dtype)
    gd_ref[...] = lax.dot_general(h_ref[...], y_ref[...], tn, preferred_element_type=jnp.float32).astype(gd_ref.dtype)


def backward_rows(pair, w_gate, w_up):
    rows, ff = pair.shape[1], pair.shape[2]
    cols = w_gate.shape[0]
    tile = 1024 if ff % 1024 == 0 else ff

    def plane(p):
        return pl.BlockSpec((None, rows, tile), lambda k: (p, 0, k))

    return pl.pallas_call(
        _rows_body,
        grid=(ff // tile,),
        in_specs=[
            plane(1),
            plane(0),
            pl.BlockSpec((cols, tile), lambda k: (0, k)),
            pl.BlockSpec((cols, tile), lambda k: (0, k)),
        ],
        out_specs=pl.BlockSpec((cols, rows), lambda k: (0, 0)),
        out_shape=jax.ShapeDtypeStruct((cols, rows), jnp.float32),
        compiler_params=pltpu.CompilerParams(dimension_semantics=("arbitrary",)),
        cost_estimate=pl.CostEstimate(
            flops=4 * rows * ff * cols, transcendentals=0,
            bytes_accessed=2 * (2 * cols * ff + 2 * rows * ff) + 4 * rows * cols),
    )(pair, pair, w_gate, w_up)


def backward_grads(pair, hidden, rows_in, rows_grad):
    rows, ff = pair.shape[1], pair.shape[2]
    cols = rows_in.shape[1]
    tile = 1024 if ff % 1024 == 0 else ff
    bf = jnp.bfloat16

    def plane(p):
        return pl.BlockSpec((None, rows, tile), lambda k: (p, 0, k))

    return pl.pallas_call(
        _grads_body,
        grid=(ff // tile,),
        in_specs=[
            plane(1),
            plane(0),
            pl.BlockSpec((None, rows, tile), lambda k: (0, 0, k)),
            pl.BlockSpec((rows, cols), lambda k: (0, 0)),
            pl.BlockSpec((rows, cols), lambda k: (0, 0)),
        ],
        out_specs=[
            pl.BlockSpec((cols, tile), lambda k: (0, k)),
            pl.BlockSpec((cols, tile), lambda k: (0, k)),
            pl.BlockSpec((tile, cols), lambda k: (k, 0)),
        ],
        out_shape=[
            jax.ShapeDtypeStruct((cols, ff), bf),
            jax.ShapeDtypeStruct((cols, ff), bf),
            jax.ShapeDtypeStruct((ff, cols), bf),
        ],
        compiler_params=pltpu.CompilerParams(dimension_semantics=("parallel",)),
        cost_estimate=pl.CostEstimate(
            flops=6 * rows * ff * cols, transcendentals=0,
            bytes_accessed=2 * (3 * cols * ff + 3 * rows * ff + 2 * rows * cols)),
    )(pair, pair, hidden, rows_in, rows_grad)


def on_device(inputs, grad_out, labels, w_gate, w_up, w_down):
    members = lax.axis_size("expert")
    replicas = lax.axis_size("dp")
    group = members // EXPERTS
    tok_count = inputs.shape[0]
    width = inputs.shape[1]
    columns = width // replicas
    capacity = 3 * tok_count // (2 * EXPERTS)
    label_col = labels[:, 0]
    onehot = (label_col[:, None] == jnp.arange(EXPERTS, dtype=jnp.int32)[None, :]).astype(jnp.int32)
    before = jnp.cumsum(onehot, axis=0) - onehot
    rank_in = jnp.sum(before * onehot, axis=1)
    slot_ids = label_col * capacity + rank_in

    both = jnp.stack([inputs, grad_out])
    slots = jnp.zeros((2, EXPERTS * capacity, width), jnp.bfloat16).at[:, slot_ids].set(both)
    send = slots.reshape(2, EXPERTS, capacity, replicas, columns)
    send = jnp.transpose(send, (3, 1, 0, 2, 4))
    send = jnp.broadcast_to(
        send[:, :, None], (replicas, EXPERTS, group, 2, capacity, columns)
    ).reshape(replicas * members, 2 * capacity * columns)
    recv = lax.all_to_all(send, ALL, 0, 0, tiled=True)
    recv = recv.reshape(replicas * members, 2, capacity, columns)
    rows_in = recv[:, 0].reshape(-1, columns)
    rows_grad = recv[:, 1].reshape(-1, columns)

    parts = forward_parts(rows_in, rows_grad, w_gate, w_up, w_down)
    reduced = lax.psum_scatter(parts, "dp", scatter_dimension=2, tiled=True)
    pair, hidden = nonlinear_stacks(reduced)
    pair = lax.all_gather(pair, "dp", axis=2, tiled=True)
    hidden = lax.all_gather(hidden, "dp", axis=2, tiled=True)

    d_rows = backward_rows(pair, w_gate, w_up).T
    back = d_rows.astype(jnp.bfloat16).reshape(replicas * members, capacity * columns)
    back = lax.all_to_all(back, ALL, 0, 0, tiled=True)
    back = back.reshape(replicas, EXPERTS, group, capacity, columns).astype(jnp.float32)
    summed = jnp.sum(back, axis=2)
    summed = jnp.transpose(summed, (1, 2, 0, 3)).reshape(EXPERTS * capacity, width)
    grad_in = summed[slot_ids].astype(jnp.bfloat16)
    grad_gate, grad_up, grad_down = backward_grads(pair, hidden, rows_in, rows_grad)
    return (grad_in, grad_gate, grad_up, grad_down)


def solution(mesh):
    return jax.shard_map(
        on_device,
        mesh=mesh,
        in_specs=(
            P(ALL, None),
            P(ALL, None),
            P(ALL, None),
            P("dp", "expert"),
            P("dp", "expert"),
            P("expert", "dp"),
        ),
        out_specs=(
            P(ALL, None),
            P("dp", "expert"),
            P("dp", "expert"),
            P("expert", "dp"),
        ),
        check_vma=False,
    )
```

```python
import jax
import jax.numpy as jnp
from jax import lax
from jax.sharding import PartitionSpec as P
from jax.experimental import pallas as pl
from jax.experimental.pallas import tpu as pltpu

EXPERTS = 8
ALL = ("dp", "expert")


def nonlinear(gate, up, dhid):
    sig = jax.nn.sigmoid(gate)
    act = gate * sig
    hidden = (act * up).astype(jnp.bfloat16)
    d_up = (dhid * act).astype(jnp.bfloat16)
    d_gate = (dhid * up * sig * (1.0 + gate * (1.0 - sig))).astype(jnp.bfloat16)
    return (hidden, d_up, d_gate)


def contract_rows(left, right):
    return lax.dot_general(
        left, right, (((0,), (0,)), ((), ())), preferred_element_type=jnp.float32
    )


def _nonlinear_body(r_ref, pair_ref, h_ref):
    gate = r_ref[0].astype(jnp.float32)
    up = r_ref[1].astype(jnp.float32)
    dhid = r_ref[2].astype(jnp.float32)
    sig = 1.0 / (1.0 + jnp.exp(-gate))
    act = gate * sig
    h_ref[0] = (act * up).astype(h_ref.dtype)
    pair_ref[0] = (dhid * act).astype(pair_ref.dtype)
    pair_ref[1] = (dhid * up * sig * (1.0 + gate * (1.0 - sig))).astype(pair_ref.dtype)


def nonlinear_stacks(reduced):
    _, rows, n = reduced.shape
    return pl.pallas_call(
        _nonlinear_body,
        out_shape=[
            jax.ShapeDtypeStruct((2, rows, n), jnp.bfloat16),
            jax.ShapeDtypeStruct((1, rows, n), jnp.bfloat16),
        ],
    )(reduced)


def _fwd_body(x_ref, y_ref, wg_ref, wu_ref, wd_ref, out_ref):
    x = x_ref[...]
    nt = (((1,), (1,)), ((), ()))
    out_ref[0] = jnp.dot(x, wg_ref[...], preferred_element_type=jnp.float32).astype(out_ref.dtype)
    out_ref[1] = jnp.dot(x, wu_ref[...], preferred_element_type=jnp.float32).astype(out_ref.dtype)
    out_ref[2] = lax.dot_general(
        y_ref[...], wd_ref[...], nt, preferred_element_type=jnp.float32
    ).astype(out_ref.dtype)


def forward_parts(rows_in, rows_grad, w_gate, w_up, w_down):
    rows, cols = rows_in.shape
    ff = w_gate.shape[1]
    tile = 1024 if ff % 1024 == 0 else ff
    return pl.pallas_call(
        _fwd_body,
        grid=(ff // tile,),
        in_specs=[
            pl.BlockSpec((rows, cols), lambda k: (0, 0)),
            pl.BlockSpec((rows, cols), lambda k: (0, 0)),
            pl.BlockSpec((cols, tile), lambda k: (0, k)),
            pl.BlockSpec((cols, tile), lambda k: (0, k)),
            pl.BlockSpec((tile, cols), lambda k: (k, 0)),
        ],
        out_specs=pl.BlockSpec((3, rows, tile), lambda k: (0, 0, k)),
        out_shape=jax.ShapeDtypeStruct((3, rows, ff), jnp.bfloat16),
        compiler_params=pltpu.CompilerParams(dimension_semantics=("parallel",)),
        cost_estimate=pl.CostEstimate(
            flops=6 * rows * ff * cols, transcendentals=0,
            bytes_accessed=2 * (3 * cols * ff + 3 * rows * ff + 2 * rows * cols)),
    )(rows_in, rows_grad, w_gate, w_up, w_down)


def _rows_body(dg_ref, du_ref, wg_ref, wu_ref, drows_ref):
    @pl.when(pl.program_id(0) == 0)
    def _():
        drows_ref[...] = jnp.zeros_like(drows_ref)
    nt = (((1,), (1,)), ((), ()))
    drows_ref[...] += lax.dot_general(
        wg_ref[...], dg_ref[...], nt, preferred_element_type=jnp.float32
    ) + lax.dot_general(wu_ref[...], du_ref[...], nt, preferred_element_type=jnp.float32)


def _grads_body(dg_ref, du_ref, h_ref, x_ref, y_ref, gg_ref, gu_ref, gd_ref):
    tn = (((0,), (0,)), ((), ()))
    x = x_ref[...]
    gg_ref[...] = lax.dot_general(x, dg_ref[...], tn, preferred_element_type=jnp.float32).astype(gg_ref.dtype)
    gu_ref[...] = lax.dot_general(x, du_ref[...], tn, preferred_element_type=jnp.float32).astype(gu_ref.dtype)
    gd_ref[...] = lax.dot_general(h_ref[...], y_ref[...], tn, preferred_element_type=jnp.float32).astype(gd_ref.dtype)


def backward_rows(pair, w_gate, w_up):
    rows, ff = pair.shape[1], pair.shape[2]
    cols = w_gate.shape[0]
    tile = 1024 if ff % 1024 == 0 else ff

    def plane(p):
        return pl.BlockSpec((None, rows, tile), lambda k: (p, 0, k))

    return pl.pallas_call(
        _rows_body,
        grid=(ff // tile,),
        in_specs=[
            plane(1),
            plane(0),
            pl.BlockSpec((cols, tile), lambda k: (0, k)),
            pl.BlockSpec((cols, tile), lambda k: (0, k)),
        ],
        out_specs=pl.BlockSpec((cols, rows), lambda k: (0, 0)),
        out_shape=jax.ShapeDtypeStruct((cols, rows), jnp.float32),
        compiler_params=pltpu.CompilerParams(dimension_semantics=("arbitrary",)),
        cost_estimate=pl.CostEstimate(
            flops=4 * rows * ff * cols, transcendentals=0,
            bytes_accessed=2 * (2 * cols * ff + 2 * rows * ff) + 4 * rows * cols),
    )(pair, pair, w_gate, w_up)


def backward_grads(pair, hidden, rows_in, rows_grad):
    rows, ff = pair.shape[1], pair.shape[2]
    cols = rows_in.shape[1]
    tile = 1024 if ff % 1024 == 0 else ff
    bf = jnp.bfloat16

    def plane(p):
        return pl.BlockSpec((None, rows, tile), lambda k: (p, 0, k))

    return pl.pallas_call(
        _grads_body,
        grid=(ff // tile,),
        in_specs=[
            plane(1),
            plane(0),
            pl.BlockSpec((None, rows, tile), lambda k: (0, 0, k)),
            pl.BlockSpec((rows, cols), lambda k: (0, 0)),
            pl.BlockSpec((rows, cols), lambda k: (0, 0)),
        ],
        out_specs=[
            pl.BlockSpec((cols, tile), lambda k: (0, k)),
            pl.BlockSpec((cols, tile), lambda k: (0, k)),
            pl.BlockSpec((tile, cols), lambda k: (k, 0)),
        ],
        out_shape=[
            jax.ShapeDtypeStruct((cols, ff), bf),
            jax.ShapeDtypeStruct((cols, ff), bf),
            jax.ShapeDtypeStruct((ff, cols), bf),
        ],
        compiler_params=pltpu.CompilerParams(dimension_semantics=("parallel",)),
        cost_estimate=pl.CostEstimate(
            flops=6 * rows * ff * cols, transcendentals=0,
            bytes_accessed=2 * (3 * cols * ff + 3 * rows * ff + 2 * rows * cols)),
    )(pair, pair, hidden, rows_in, rows_grad)


def on_device(inputs, grad_out, labels, w_gate, w_up, w_down):
    members = lax.axis_size("expert")
    replicas = lax.axis_size("dp")
    group = members // EXPERTS
    tok_count = inputs.shape[0]
    width = inputs.shape[1]
    columns = width // replicas
    capacity = 3 * tok_count // (2 * EXPERTS)
    label_col = labels[:, 0]
    onehot = (label_col[:, None] == jnp.arange(EXPERTS, dtype=jnp.int32)[None, :]).astype(jnp.int32)
    before = jnp.cumsum(onehot, axis=0) - onehot
    rank_in = jnp.sum(before * onehot, axis=1)
    slot_ids = label_col * capacity + rank_in

    both = jnp.stack([inputs, grad_out])
    slots = jnp.zeros((2, EXPERTS * capacity, width), jnp.bfloat16).at[:, slot_ids].set(both)
    send = slots.reshape(2, EXPERTS, capacity, replicas, columns)
    send = jnp.transpose(send, (3, 1, 0, 2, 4))
    send = jnp.broadcast_to(
        send[:, :, None], (replicas, EXPERTS, group, 2, capacity, columns)
    ).reshape(replicas * members, 2, capacity * columns)
    recv = lax.all_to_all(send, ALL, 0, 0, tiled=True)
    recv = recv.reshape(replicas * members, 2, capacity, columns)
    rows_in = recv[:, 0].reshape(-1, columns)
    rows_grad = recv[:, 1].reshape(-1, columns)

    parts = forward_parts(rows_in, rows_grad, w_gate, w_up, w_down)
    reduced = lax.psum_scatter(parts, "dp", scatter_dimension=2, tiled=True)
    pair, hidden = nonlinear_stacks(reduced)
    pair = lax.all_gather(pair, "dp", axis=2, tiled=True)
    hidden = lax.all_gather(hidden, "dp", axis=2, tiled=True)

    d_rows = backward_rows(pair, w_gate, w_up).T
    back = d_rows.astype(jnp.bfloat16).reshape(replicas * members, capacity * columns)
    back = lax.all_to_all(back, ALL, 0, 0, tiled=True)
    back = back.reshape(replicas, EXPERTS, group, capacity, columns).astype(jnp.float32)
    summed = jnp.sum(back, axis=2)
    summed = jnp.transpose(summed, (1, 2, 0, 3)).reshape(EXPERTS * capacity, width)
    grad_in = summed[slot_ids].astype(jnp.bfloat16)
    grad_gate, grad_up, grad_down = backward_grads(pair, hidden, rows_in, rows_grad)
    return (grad_in, grad_gate, grad_up, grad_down)


def solution(mesh):
    return jax.shard_map(
        on_device,
        mesh=mesh,
        in_specs=(
            P(ALL, None),
            P(ALL, None),
            P(ALL, None),
            P("dp", "expert"),
            P("dp", "expert"),
            P("expert", "dp"),
        ),
        out_specs=(
            P(ALL, None),
            P("dp", "expert"),
            P("dp", "expert"),
            P("expert", "dp"),
        ),
        check_vma=False,
    )
```
